512 devices in a mesh: rep: 4 (over z_hi), exp: 16 (over x, y), mdl: 8 (over z_lo, core).
Axes of the slice: x: 4, y: 4, z: 16 (z_hi: 4, z_lo: 4; z = z_hi * 4 + z_lo), core: 2. Of those that a mesh axis runs over, the one named last changes fastest.
Arguments:
- inner_experts: bfloat16 [4, 16, 2, 768, 2048], P('rep', 'exp', None, None, 'mdl'), may hold values from -6 to 6
- inner_dense: bfloat16 [4, 9216, 768], P('rep', ('exp', 'mdl')), may hold values from -6 to 6
- inner_small: bfloat16 [4, 18, 768], P('rep'), may hold values from -6 to 6
- inner_embed: bfloat16 [4, 8192, 768], P('rep', ('exp', 'mdl')), may hold values from -6 to 6
- outer_experts: float32 [16, 2, 768, 2048], P('exp', None, ('rep', 'mdl')), may hold values from -6 to 6
- outer_dense: float32 [9216, 768], P(('exp', 'mdl'), 'rep'), may hold values from -6 to 6
- outer_small: float32 [18, 768], P(None, 'rep'), may hold values from -6 to 6
- outer_embed: float32 [8192, 768], P(('exp', 'mdl'), 'rep'), may hold values from -6 to 6
- moment_experts: float32 [16, 2, 768, 2048], P('exp', None, ('rep', 'mdl')), may hold values from -3 to 3
- moment_dense: float32 [9216, 768], P(('exp', 'mdl'), 'rep'), may hold values from -3 to 3
- moment_small: float32 [18, 768], P(None, 'rep'), may hold values from -3 to 3
- moment_embed: float32 [8192, 768], P(('exp', 'mdl'), 'rep'), may hold values from -3 to 3
- embed_basis: float32 [768, 64], replicated, may hold values from -0.21875 to 0.21875
Outputs:
- new_outer_experts: float32 [16, 2, 768, 2048], P('exp', None, ('rep', 'mdl'))
- new_moment_experts: float32 [16, 2, 768, 2048], P('exp', None, ('rep', 'mdl'))
- copy_experts: bfloat16 [16, 2, 768, 2048], P('exp', None, None, 'mdl')
- new_outer_dense: float32 [9216, 768], P(('exp', 'mdl'), 'rep')
- new_moment_dense: float32 [9216, 768], P(('exp', 'mdl'), 'rep')
- copy_dense: bfloat16 [9216, 768], P(('exp', 'mdl'))
- new_outer_small: float32 [18, 768], P(None, 'rep')
- new_moment_small: float32 [18, 768], P(None, 'rep')
- copy_small: bfloat16 [18, 768], replicated
- new_outer_embed: float32 [8192, 768], P(('exp', 'mdl'), 'rep')
- new_moment_embed: float32 [8192, 768], P(('exp', 'mdl'), 'rep')
- copy_embed: bfloat16 [8192, 768], P(('exp', 'mdl'))
The draws below stay inside these ranges and needn't reach their ends.
All inputs are finite; a program needn't handle non-finite values.
Results may differ from the reference program's by a relative error of at most 0.012.
Values may be sent and summed in bfloat16 or wider, within the bound.
No kernel may reach another device: no remote copies, remote signals or barrier semaphores. Data moves between devices by JAX's collectives and lax.ppermute only.
A program may use at most 64 MiB of HBM per device.

```python
import jax
import jax.numpy as jnp
from jax import lax

D = 768
FF = 2048
E = 16
RANK = 64
V = 8192
DENSE_ROWS = 9216
SMALL_ROWS = 18
N_REP = 4


def level_of(key, shape, shards, least, top_value):
    def one(position, shards_of):
        heights = jax.random.uniform(jax.random.fold_in(jax.random.fold_in(key, 6), position), (shards_of,), jnp.float32, least / len(shards), top_value / len(shards))
        return jnp.repeat(jnp.exp(heights), shape[position] // shards_of).reshape((-1,) + (1,) * (len(shape) - position - 1))

    level = one(*shards[0])
    for cut in shards[1:]:
        level = level * one(*cut)
    return level


def centred(stream_key, shape, spread, limit, split=(), kind=jnp.bfloat16):
    array = spread * jax.random.normal(stream_key, shape, jnp.float32)
    if split:
        array = array * level_of(stream_key, shape, split, -0.22, 0.18)
    return jnp.clip(array, -limit, limit).astype(kind)


def setup_inputs(seed: int = 0) -> dict:
    key_of = jax.random.split(jax.random.key(seed), 14)
    inner_experts = centred(key_of[0], (N_REP, E, 2, D, FF), 1.0, 6.0, ((0, 4), (1, 16), (4, 8)))
    inner_dense = centred(key_of[1], (N_REP, DENSE_ROWS, D), 1.0, 6.0, ((0, 4), (1, 128)))
    inner_small = centred(key_of[2], (N_REP, SMALL_ROWS, D), 1.0, 6.0, ((0, 4),))
    inner_embed = centred(key_of[3], (N_REP, V, D), 1.0, 6.0, ((0, 4), (1, 128)))
    outer_experts = centred(key_of[4], (E, 2, D, FF), 1.0, 6.0, ((0, 16), (2, 32)), jnp.float32)
    outer_dense = centred(key_of[5], (DENSE_ROWS, D), 1.0, 6.0, ((0, 128), (1, 4)), jnp.float32)
    outer_small = centred(key_of[6], (SMALL_ROWS, D), 1.0, 6.0, ((1, 4),), jnp.float32)
    outer_embed = centred(key_of[7], (V, D), 1.0, 6.0, ((0, 128), (1, 4)), jnp.float32)
    moment_experts = centred(key_of[8], (E, 2, D, FF), 0.5, 3.0, ((0, 16), (2, 32)), jnp.float32)
    moment_dense = centred(key_of[9], (DENSE_ROWS, D), 0.5, 3.0, ((0, 128), (1, 4)), jnp.float32)
    moment_small = centred(key_of[10], (SMALL_ROWS, D), 0.5, 3.0, ((1, 4),), jnp.float32)
    moment_embed = centred(key_of[11], (V, D), 0.5, 3.0, ((0, 128), (1, 4)), jnp.float32)
    embed_basis = centred(key_of[12], (D, RANK), D ** -0.5, 0.21875, (), jnp.float32)
    return dict(inner_experts=inner_experts, inner_dense=inner_dense, inner_small=inner_small, inner_embed=inner_embed, outer_experts=outer_experts, outer_dense=outer_dense, outer_small=outer_small, outer_embed=outer_embed, moment_experts=moment_experts, moment_dense=moment_dense, moment_small=moment_small, moment_embed=moment_embed, embed_basis=embed_basis)


decay_rate = 0.5
outer_rate = 0.7


def nesterov(outer, moment, grad_value):
    moment_new = decay_rate * moment + grad_value
    outer_new = outer - outer_rate * (grad_value + decay_rate * moment_new)
    return outer_new, moment_new, outer_new.astype(jnp.bfloat16)


def reference(inner_experts, inner_dense, inner_small, inner_embed, outer_experts, outer_dense, outer_small, outer_embed, moment_experts, moment_dense, moment_small, moment_embed, embed_basis):
    grad_experts = outer_experts - jnp.sum(inner_experts, axis=0, dtype=jnp.float32) / N_REP
    grad_dense = outer_dense - jnp.sum(inner_dense, axis=0, dtype=jnp.float32) / N_REP
    grad_small = outer_small - jnp.sum(inner_small, axis=0, dtype=jnp.float32) / N_REP
    mean_embed = jnp.sum(inner_embed, axis=0, dtype=jnp.float32) / N_REP
    coefficient = jnp.dot(outer_embed - mean_embed, embed_basis, precision=lax.Precision.HIGHEST, preferred_element_type=jnp.float32)
    grad_embed = jnp.dot(coefficient, embed_basis.T, precision=lax.Precision.HIGHEST, preferred_element_type=jnp.float32)
    expert_new = nesterov(outer_experts, moment_experts, grad_experts)
    dense_new = nesterov(outer_dense, moment_dense, grad_dense)
    small_new = nesterov(outer_small, moment_small, grad_small)
    embed_new = nesterov(outer_embed, moment_embed, grad_embed)
    return (expert_new[0], expert_new[1], expert_new[2], dense_new[0], dense_new[1], dense_new[2], small_new[0], small_new[1], small_new[2], embed_new[0], embed_new[1], embed_new[2])
```

```python
import jax
import jax.numpy as jnp
from jax import lax
from jax.sharding import PartitionSpec as P

decay_rate = 0.5
outer_rate = 0.7


def nesterov(outer, moment, grad_value):
    moment_new = decay_rate * moment + grad_value
    outer_new = outer - outer_rate * (grad_value + decay_rate * moment_new)
    return (outer_new, moment_new)


def split_rows(x, parts):
    rows, cols = x.shape
    return x.reshape(rows, parts, cols // parts).transpose(1, 0, 2).reshape(parts, -1)


def on_device(
    inner_experts,
    inner_dense,
    inner_small,
    inner_embed,
    outer_experts,
    outer_dense,
    outer_small,
    outer_embed,
    moment_experts,
    moment_dense,
    moment_small,
    moment_embed,
    embed_basis,
):
    groups = lax.axis_size("rep")
    hi_prec = lax.Precision.HIGHEST

    own_shard = inner_experts[0, 0]
    halves, all_rows, my_cols = own_shard.shape
    rep_rows = all_rows // groups
    ex_send = (
        own_shard.reshape(halves, groups, rep_rows, my_cols)
        .transpose(1, 0, 2, 3)
        .reshape(groups, -1)
    )
    de_send = split_rows(inner_dense[0], groups)
    sm_send = split_rows(inner_small[0], groups)

    col_count = outer_embed.shape[1]
    offset = lax.axis_index("rep") * col_count
    basis_part = lax.dynamic_slice_in_dim(embed_basis, offset, col_count, 0)
    partial_value = jnp.dot(
        outer_embed, basis_part, precision=hi_prec, preferred_element_type=jnp.float32
    ) - jnp.dot(
        inner_embed[0].astype(jnp.float32),
        embed_basis,
        precision=hi_prec,
        preferred_element_type=jnp.float32,
    ) / groups
    part_hi = partial_value.astype(jnp.bfloat16)
    part_lo = (partial_value - part_hi.astype(jnp.float32)).astype(jnp.bfloat16)
    pp = jnp.concatenate([part_hi.reshape(-1), part_lo.reshape(-1)])
    pp_send = jnp.broadcast_to(pp[None], (groups, pp.shape[0]))

    sizes = [ex_send.shape[1], de_send.shape[1], sm_send.shape[1], pp.shape[0]]
    send = jnp.concatenate([ex_send, de_send, sm_send, pp_send], axis=1)
    recv = lax.all_to_all(send, "rep", split_axis=0, concat_axis=0, tiled=True)
    bounds = [0]
    for s in sizes:
        bounds.append(bounds[-1] + s)
    parts = [recv[:, bounds[i] : bounds[i + 1]] for i in range(4)]

    ex_sum = jnp.sum(parts[0].astype(jnp.float32), axis=0).reshape(halves, rep_rows, my_cols)
    dense_sum = jnp.sum(parts[1].astype(jnp.float32), axis=0).reshape(outer_dense.shape)
    small_sum = jnp.sum(parts[2].astype(jnp.float32), axis=0).reshape(outer_small.shape)
    pp_recv = parts[3].astype(jnp.float32)
    nco = partial_value.size
    coefficient = jnp.sum(pp_recv[:, :nco] + pp_recv[:, nco:], axis=0).reshape(
        partial_value.shape
    )

    expert_sum = lax.all_to_all(ex_sum, "mdl", split_axis=1, concat_axis=2, tiled=True)
    grad_experts = outer_experts[0] - expert_sum / groups
    grad_dense = outer_dense - dense_sum / groups
    grad_small = outer_small - small_sum / groups
    grad_embed = jnp.dot(
        coefficient, basis_part.T, precision=hi_prec, preferred_element_type=jnp.float32
    )
    expert_outer, expert_moment = nesterov(outer_experts[0], moment_experts[0], grad_experts)
    dense_outer, dense_moment = nesterov(outer_dense, moment_dense, grad_dense)
    small_outer, small_moment = nesterov(outer_small, moment_small, grad_small)
    embed_outer, embed_moment = nesterov(outer_embed, moment_embed, grad_embed)
    spread = lax.all_to_all(
        expert_outer.astype(jnp.bfloat16), "mdl", split_axis=2, concat_axis=1, tiled=True
    )

    pieces = [
        spread,
        dense_outer.astype(jnp.bfloat16),
        small_outer.astype(jnp.bfloat16),
        embed_outer.astype(jnp.bfloat16),
    ]
    flat = jnp.concatenate([p.reshape(-1) for p in pieces])
    gathered = lax.all_gather(flat, "rep", axis=0, tiled=False)
    outs = []
    start = 0
    for p in pieces:
        n = p.size
        g = gathered[:, start : start + n].reshape((groups,) + p.shape)
        start += n
        if p.ndim == 3:
            g = g.transpose(1, 0, 2, 3).reshape(p.shape[0], groups * p.shape[1], p.shape[2])
        else:
            g = g.transpose(1, 0, 2).reshape(p.shape[0], groups * p.shape[1])
        outs.append(g)

    return (
        expert_outer[None],
        expert_moment[None],
        outs[0][None],
        dense_outer,
        dense_moment,
        outs[1],
        small_outer,
        small_moment,
        outs[2],
        embed_outer,
        embed_moment,
        outs[3],
    )


def solution(mesh):
    placed = (
        P("rep", "exp", None, None, "mdl"),
        P("rep", ("exp", "mdl"), None),
        P("rep", None, None),
        P("rep", ("exp", "mdl"), None),
        P("exp", None, ("rep", "mdl"), None),
        P(("exp", "mdl"), "rep"),
        P(None, "rep"),
        P(("exp", "mdl"), "rep"),
        P("exp", None, ("rep", "mdl"), None),
        P(("exp", "mdl"), "rep"),
        P(None, "rep"),
        P(("exp", "mdl"), "rep"),
        P(),
    )
    return jax.shard_map(
        on_device,
        mesh=mesh,
        in_specs=placed,
        out_specs=(
            P("exp", None, ("rep", "mdl"), None),
            P("exp", None, ("rep", "mdl"), None),
            P("exp", None, None, "mdl"),
            P(("exp", "mdl"), "rep"),
            P(("exp", "mdl"), "rep"),
            P(("exp", "mdl"), None),
            P(None, "rep"),
            P(None, "rep"),
            P(),
            P(("exp", "mdl"), "rep"),
            P(("exp", "mdl"), "rep"),
            P(("exp", "mdl"), None),
        ),
        check_vma=False,
    )
```

```python
import jax
import jax.numpy as jnp
from jax import lax
from jax.sharding import PartitionSpec as P

decay_rate = 0.5
outer_rate = 0.7


def nesterov(outer, moment, grad_value):
    moment_new = decay_rate * moment + grad_value
    outer_new = outer - outer_rate * (grad_value + decay_rate * moment_new)
    return (outer_new, moment_new)


def split_rows(x, parts):
    rows, cols = x.shape
    return x.reshape(rows, parts, cols // parts).transpose(1, 0, 2).reshape(parts, -1)


def to_next(x, groups):
    return lax.ppermute(x, "rep", [(i, (i + 1) % groups) for i in range(groups)])


def to_prev(x, groups):
    return lax.ppermute(x, "rep", [(i, (i - 1) % groups) for i in range(groups)])


def rep_exchange(send, groups):
    assert groups == 4
    me = lax.axis_index("rep")
    rel = [lax.dynamic_index_in_dim(send, (me + d) % groups, 0, False) for d in range(groups)]
    k = send.shape[1]
    half = k // 2
    fwd = to_next(jnp.concatenate([rel[1], rel[2][:half]]), groups)
    bwd = to_prev(jnp.concatenate([rel[3], rel[2][half:]]), groups)
    far_a = to_next(fwd[k:], groups)
    far_b = to_prev(bwd[k:], groups)
    far = jnp.concatenate([far_a, far_b])
    return jnp.stack([rel[0], fwd[:k], bwd[:k], far])


def rep_gather(flat, groups):
    assert groups == 4
    me = lax.axis_index("rep")
    n = flat.shape[0]
    half = n // 2
    from_prev = to_next(flat, groups)
    from_next = to_prev(flat, groups)
    far_a = to_next(from_prev[:half], groups)
    far_b = to_prev(from_next[half:], groups)
    far = jnp.concatenate([far_a, far_b])
    out = jnp.zeros((groups, n), flat.dtype)
    for d, row in enumerate([flat, from_next, far, from_prev]):
        out = lax.dynamic_update_index_in_dim(out, row, (me + d) % groups, 0)
    return out


def on_device(
    inner_experts,
    inner_dense,
    inner_small,
    inner_embed,
    outer_experts,
    outer_dense,
    outer_small,
    outer_embed,
    moment_experts,
    moment_dense,
    moment_small,
    moment_embed,
    embed_basis,
):
    groups = lax.axis_size("rep")
    hi_prec = lax.Precision.HIGHEST

    own_shard = inner_experts[0, 0]
    halves, all_rows, my_cols = own_shard.shape
    rep_rows = all_rows // groups
    ex_send = (
        own_shard.reshape(halves, groups, rep_rows, my_cols)
        .transpose(1, 0, 2, 3)
        .reshape(groups, -1)
    )
    de_send = split_rows(inner_dense[0], groups)
    sm_send = split_rows(inner_small[0], groups)

    col_count = outer_embed.shape[1]
    offset = lax.axis_index("rep") * col_count
    basis_part = lax.dynamic_slice_in_dim(embed_basis, offset, col_count, 0)
    partial_value = jnp.dot(
        outer_embed, basis_part, precision=hi_prec, preferred_element_type=jnp.float32
    ) - jnp.dot(
        inner_embed[0].astype(jnp.float32),
        embed_basis,
        precision=hi_prec,
        preferred_element_type=jnp.float32,
    ) / groups
    part_hi = partial_value.astype(jnp.bfloat16)
    part_lo = (partial_value - part_hi.astype(jnp.float32)).astype(jnp.bfloat16)
    pp = jnp.concatenate([part_hi.reshape(-1), part_lo.reshape(-1)])
    pp_send = jnp.broadcast_to(pp[None], (groups, pp.shape[0]))

    sizes = [ex_send.shape[1], de_send.shape[1], sm_send.shape[1], pp.shape[0]]
    send = jnp.concatenate([ex_send, de_send, sm_send, pp_send], axis=1)
    recv = rep_exchange(send, groups)
    bounds = [0]
    for s in sizes:
        bounds.append(bounds[-1] + s)
    parts = [recv[:, bounds[i] : bounds[i + 1]] for i in range(4)]

    ex_sum = jnp.sum(parts[0].astype(jnp.float32), axis=0).reshape(halves, rep_rows, my_cols)
    dense_sum = jnp.sum(parts[1].astype(jnp.float32), axis=0).reshape(outer_dense.shape)
    small_sum = jnp.sum(parts[2].astype(jnp.float32), axis=0).reshape(outer_small.shape)
    pp_recv = parts[3].astype(jnp.float32)
    nco = partial_value.size
    coefficient = jnp.sum(pp_recv[:, :nco] + pp_recv[:, nco:], axis=0).reshape(
        partial_value.shape
    )

    expert_sum = lax.all_to_all(ex_sum, "mdl", split_axis=1, concat_axis=2, tiled=True)
    grad_experts = outer_experts[0] - expert_sum / groups
    grad_dense = outer_dense - dense_sum / groups
    grad_small = outer_small - small_sum / groups
    grad_embed = jnp.dot(
        coefficient, basis_part.T, precision=hi_prec, preferred_element_type=jnp.float32
    )
    expert_outer, expert_moment = nesterov(outer_experts[0], moment_experts[0], grad_experts)
    dense_outer, dense_moment = nesterov(outer_dense, moment_dense, grad_dense)
    small_outer, small_moment = nesterov(outer_small, moment_small, grad_small)
    embed_outer, embed_moment = nesterov(outer_embed, moment_embed, grad_embed)
    spread = lax.all_to_all(
        expert_outer.astype(jnp.bfloat16), "mdl", split_axis=2, concat_axis=1, tiled=True
    )

    pieces = [
        spread,
        dense_outer.astype(jnp.bfloat16),
        small_outer.astype(jnp.bfloat16),
        embed_outer.astype(jnp.bfloat16),
    ]
    flat = jnp.concatenate([p.reshape(-1) for p in pieces])
    gathered = rep_gather(flat, groups)
    outs = []
    start = 0
    for p in pieces:
        n = p.size
        g = gathered[:, start : start + n].reshape((groups,) + p.shape)
        start += n
        if p.ndim == 3:
            g = g.transpose(1, 0, 2, 3).reshape(p.shape[0], groups * p.shape[1], p.shape[2])
        else:
            g = g.transpose(1, 0, 2).reshape(p.shape[0], groups * p.shape[1])
        outs.append(g)

    return (
        expert_outer[None],
        expert_moment[None],
        outs[0][None],
        dense_outer,
        dense_moment,
        outs[1],
        small_outer,
        small_moment,
        outs[2],
        embed_outer,
        embed_moment,
        outs[3],
    )


def solution(mesh):
    placed = (
        P("rep", "exp", None, None, "mdl"),
        P("rep", ("exp", "mdl"), None),
        P("rep", None, None),
        P("rep", ("exp", "mdl"), None),
        P("exp", None, ("rep", "mdl"), None),
        P(("exp", "mdl"), "rep"),
        P(None, "rep"),
        P(("exp", "mdl"), "rep"),
        P("exp", None, ("rep", "mdl"), None),
        P(("exp", "mdl"), "rep"),
        P(None, "rep"),
        P(("exp", "mdl"), "rep"),
        P(),
    )
    return jax.shard_map(
        on_device,
        mesh=mesh,
        in_specs=placed,
        out_specs=(
            P("exp", None, ("rep", "mdl"), None),
            P("exp", None, ("rep", "mdl"), None),
            P("exp", None, None, "mdl"),
            P(("exp", "mdl"), "rep"),
            P(("exp", "mdl"), "rep"),
            P(("exp", "mdl"), None),
            P(None, "rep"),
            P(None, "rep"),
            P(),
            P(("exp", "mdl"), "rep"),
            P(("exp", "mdl"), "rep"),
            P(("exp", "mdl"), None),
        ),
        check_vma=False,
    )
```

```python
import jax
import jax.numpy as jnp
from jax import lax
from jax.sharding import PartitionSpec as P

decay_rate = 0.5
outer_rate = 0.7


def nesterov(outer, moment, grad_value):
    moment_new = decay_rate * moment + grad_value
    outer_new = outer - outer_rate * (grad_value + decay_rate * moment_new)
    return (outer_new, moment_new)


def split_rows(x, parts):
    rows, cols = x.shape
    return x.reshape(rows, parts, cols // parts).transpose(1, 0, 2).reshape(parts, -1)


def to_next(x, groups):
    return lax.ppermute(x, "rep", [(i, (i + 1) % groups) for i in range(groups)])


def to_prev(x, groups):
    return lax.ppermute(x, "rep", [(i, (i - 1) % groups) for i in range(groups)])


def rep_exchange(send, groups):
    assert groups == 4
    me = lax.axis_index("rep")
    rel = [lax.dynamic_index_in_dim(send, (me + d) % groups, 0, False) for d in range(groups)]
    k = send.shape[1]
    half = k // 2
    fwd = to_next(jnp.concatenate([rel[1], rel[2][:half]]), groups)
    bwd = to_prev(jnp.concatenate([rel[3], rel[2][half:]]), groups)
    far_a = to_next(fwd[k:], groups)
    far_b = to_prev(bwd[k:], groups)
    f32 = jnp.float32
    near = rel[0].astype(f32) + fwd[:k].astype(f32) + bwd[:k].astype(f32)
    return near + jnp.concatenate([far_a, far_b]).astype(f32)


def rep_gather(flat, groups):
    assert groups == 4
    me = lax.axis_index("rep")
    n = flat.shape[0]
    half = n // 2
    from_prev = to_next(flat, groups)
    from_next = to_prev(flat, groups)
    far_a = to_next(from_prev[:half], groups)
    far_b = to_prev(from_next[half:], groups)
    far = jnp.concatenate([far_a, far_b])
    rel = jnp.stack([flat, from_next, far, from_prev])
    return [lax.dynamic_index_in_dim(rel, (j - me) % groups, 0, False) for j in range(groups)]


def on_device(
    inner_experts,
    inner_dense,
    inner_small,
    inner_embed,
    outer_experts,
    outer_dense,
    outer_small,
    outer_embed,
    moment_experts,
    moment_dense,
    moment_small,
    moment_embed,
    embed_basis,
):
    groups = lax.axis_size("rep")
    hi_prec = lax.Precision.HIGHEST

    lanes = 128
    own_shard = inner_experts[0, 0]
    halves, all_rows, my_cols = own_shard.shape
    rep_rows = all_rows // groups
    ex_send = (
        own_shard.reshape(halves, groups, rep_rows, my_cols)
        .transpose(1, 0, 2, 3)
        .reshape(groups, -1, lanes)
    )
    de_send = split_rows(inner_dense[0], groups).reshape(groups, -1, lanes)
    sm_send = split_rows(inner_small[0], groups).reshape(groups, -1, lanes)

    col_count = outer_embed.shape[1]
    offset = lax.axis_index("rep") * col_count
    basis_part = lax.dynamic_slice_in_dim(embed_basis, offset, col_count, 0)
    partial_value = jnp.dot(
        outer_embed, basis_part, precision=hi_prec, preferred_element_type=jnp.float32
    ) - jnp.dot(
        inner_embed[0].astype(jnp.float32),
        embed_basis,
        precision=hi_prec,
        preferred_element_type=jnp.float32,
    ) / groups
    part_hi = partial_value.astype(jnp.bfloat16)
    part_lo = (partial_value - part_hi.astype(jnp.float32)).astype(jnp.bfloat16)
    pp = jnp.concatenate([part_hi.reshape(-1, lanes), part_lo.reshape(-1, lanes)])
    pp_send = jnp.broadcast_to(pp[None], (groups,) + pp.shape)

    sizes = [ex_send.shape[1], de_send.shape[1], sm_send.shape[1], pp.shape[0]]
    send = jnp.concatenate([ex_send, de_send, sm_send, pp_send], axis=1)
    total = rep_exchange(send, groups)
    bounds = [0]
    for s in sizes:
        bounds.append(bounds[-1] + s)
    parts = [total[bounds[i] : bounds[i + 1]] for i in range(4)]

    ex_sum = parts[0].reshape(halves, rep_rows, my_cols)
    dense_sum = parts[1].reshape(outer_dense.shape)
    small_sum = parts[2].reshape(outer_small.shape)
    nhalf = parts[3].shape[0] // 2
    coefficient = (parts[3][:nhalf] + parts[3][nhalf:]).reshape(partial_value.shape)

    expert_sum = lax.all_to_all(ex_sum, "mdl", split_axis=1, concat_axis=2, tiled=True)
    grad_experts = outer_experts[0] - expert_sum / groups
    grad_dense = outer_dense - dense_sum / groups
    grad_small = outer_small - small_sum / groups
    grad_embed = jnp.dot(
        coefficient, basis_part.T, precision=hi_prec, preferred_element_type=jnp.float32
    )
    expert_outer, expert_moment = nesterov(outer_experts[0], moment_experts[0], grad_experts)
    dense_outer, dense_moment = nesterov(outer_dense, moment_dense, grad_dense)
    small_outer, small_moment = nesterov(outer_small, moment_small, grad_small)
    embed_outer, embed_moment = nesterov(outer_embed, moment_embed, grad_embed)
    spread = lax.all_to_all(
        expert_outer.astype(jnp.bfloat16), "mdl", split_axis=2, concat_axis=1, tiled=True
    )

    pieces = [
        spread,
        dense_outer.astype(jnp.bfloat16),
        small_outer.astype(jnp.bfloat16),
        embed_outer.astype(jnp.bfloat16),
    ]
    flat = jnp.concatenate([p.reshape(-1, lanes) for p in pieces])
    blocks = rep_gather(flat, groups)
    outs = []
    start = 0
    for p in pieces:
        n = p.size // lanes
        g = jnp.stack([b[start : start + n] for b in blocks]).reshape((groups,) + p.shape)
        start += n
        if p.ndim == 3:
            g = g.transpose(1, 0, 2, 3).reshape(p.shape[0], groups * p.shape[1], p.shape[2])
        else:
            g = g.transpose(1, 0, 2).reshape(p.shape[0], groups * p.shape[1])
        outs.append(g)

    return (
        expert_outer[None],
        expert_moment[None],
        outs[0][None],
        dense_outer,
        dense_moment,
        outs[1],
        small_outer,
        small_moment,
        outs[2],
        embed_outer,
        embed_moment,
        outs[3],
    )


def solution(mesh):
    placed = (
        P("rep", "exp", None, None, "mdl"),
        P("rep", ("exp", "mdl"), None),
        P("rep", None, None),
        P("rep", ("exp", "mdl"), None),
        P("exp", None, ("rep", "mdl"), None),
        P(("exp", "mdl"), "rep"),
        P(None, "rep"),
        P(("exp", "mdl"), "rep"),
        P("exp", None, ("rep", "mdl"), None),
        P(("exp", "mdl"), "rep"),
        P(None, "rep"),
        P(("exp", "mdl"), "rep"),
        P(),
    )
    return jax.shard_map(
        on_device,
        mesh=mesh,
        in_specs=placed,
        out_specs=(
            P("exp", None, ("rep", "mdl"), None),
            P("exp", None, ("rep", "mdl"), None),
            P("exp", None, None, "mdl"),
            P(("exp", "mdl"), "rep"),
            P(("exp", "mdl"), "rep"),
            P(("exp", "mdl"), None),
            P(None, "rep"),
            P(None, "rep"),
            P(),
            P(("exp", "mdl"), "rep"),
            P(("exp", "mdl"), "rep"),
            P(("exp", "mdl"), None),
        ),
        check_vma=False,
    )
```

```python
import jax
import jax.numpy as jnp
from jax import lax
from jax.sharding import PartitionSpec as P

decay_rate = 0.5
outer_rate = 0.7


def nesterov(outer, moment, grad_value):
    moment_new = decay_rate * moment + grad_value
    outer_new = outer - outer_rate * (grad_value + decay_rate * moment_new)
    return (outer_new, moment_new)


def split_rows(x, parts):
    rows, cols = x.shape
    return x.reshape(rows, parts, cols // parts).transpose(1, 0, 2).reshape(parts, -1)


def to_next(x, groups):
    return lax.ppermute(x, "rep", [(i, (i + 1) % groups) for i in range(groups)])


def to_prev(x, groups):
    return lax.ppermute(x, "rep", [(i, (i - 1) % groups) for i in range(groups)])


def rep_exchange(send, raw_rows, groups):
    assert groups == 4
    me = lax.axis_index("rep")
    rel = [lax.dynamic_index_in_dim(send, (me + d) % groups, 0, False) for d in range(groups)]
    k = send.shape[1]
    m = k - raw_rows
    h = m // 2
    rh = raw_rows // 2
    f32 = jnp.float32
    bf = send.dtype
    a = to_next(jnp.concatenate([rel[2][:h], rel[2][m : m + rh]]), groups)
    b = to_prev(jnp.concatenate([rel[2][h:m], rel[2][m + rh :]]), groups)
    x = to_next(
        jnp.concatenate(
            [(rel[1][:h].astype(f32) + a[:h].astype(f32)).astype(bf), rel[1][h:], a[h:]]
        ),
        groups,
    )
    y = to_prev(
        jnp.concatenate(
            [rel[3][:h], (rel[3][h:m].astype(f32) + b[: m - h].astype(f32)).astype(bf), rel[3][m:], b[m - h :]]
        ),
        groups,
    )
    near = rel[0].astype(f32) + x[:k].astype(f32) + y[:k].astype(f32)
    far_raw = jnp.concatenate([x[k:], y[k:]]).astype(f32)
    return jnp.concatenate([near[:m], near[m:] + far_raw])


def rep_gather(flat, groups):
    assert groups == 4
    me = lax.axis_index("rep")
    n = flat.shape[0]
    half = n // 2
    from_prev = to_next(flat, groups)
    from_next = to_prev(flat, groups)
    far_a = to_next(from_prev[:half], groups)
    far_b = to_prev(from_next[half:], groups)
    far = jnp.concatenate([far_a, far_b])
    rel = jnp.stack([flat, from_next, far, from_prev])
    return [lax.dynamic_index_in_dim(rel, (j - me) % groups, 0, False) for j in range(groups)]


def on_device(
    inner_experts,
    inner_dense,
    inner_small,
    inner_embed,
    outer_experts,
    outer_dense,
    outer_small,
    outer_embed,
    moment_experts,
    moment_dense,
    moment_small,
    moment_embed,
    embed_basis,
):
    groups = lax.axis_size("rep")
    hi_prec = lax.Precision.HIGHEST

    lanes = 128
    own_shard = inner_experts[0, 0]
    halves, all_rows, my_cols = own_shard.shape
    rep_rows = all_rows // groups
    ex_send = (
        own_shard.reshape(halves, groups, rep_rows, my_cols)
        .transpose(1, 0, 2, 3)
        .reshape(groups, -1, lanes)
    )
    de_send = split_rows(inner_dense[0], groups).reshape(groups, -1, lanes)
    sm_send = split_rows(inner_small[0], groups).reshape(groups, -1, lanes)

    col_count = outer_embed.shape[1]
    offset = lax.axis_index("rep") * col_count
    basis_part = lax.dynamic_slice_in_dim(embed_basis, offset, col_count, 0)
    partial_value = jnp.dot(
        outer_embed, basis_part, precision=hi_prec, preferred_element_type=jnp.float32
    ) - jnp.dot(
        inner_embed[0].astype(jnp.float32),
        embed_basis,
        precision=hi_prec,
        preferred_element_type=jnp.float32,
    ) / groups
    part_hi = partial_value.astype(jnp.bfloat16)
    part_lo = (partial_value - part_hi.astype(jnp.float32)).astype(jnp.bfloat16)
    pp = jnp.concatenate([part_hi.reshape(-1, lanes), part_lo.reshape(-1, lanes)])
    pp_send = jnp.broadcast_to(pp[None], (groups,) + pp.shape)

    sizes = [ex_send.shape[1], de_send.shape[1], sm_send.shape[1], pp.shape[0]]
    send = jnp.concatenate([ex_send, de_send, sm_send, pp_send], axis=1)
    total = rep_exchange(send, pp.shape[0], groups)
    bounds = [0]
    for s in sizes:
        bounds.append(bounds[-1] + s)
    parts = [total[bounds[i] : bounds[i + 1]] for i in range(4)]

    ex_sum = parts[0].reshape(halves, rep_rows, my_cols)
    dense_sum = parts[1].reshape(outer_dense.shape)
    small_sum = parts[2].reshape(outer_small.shape)
    nhalf = parts[3].shape[0] // 2
    coefficient = (parts[3][:nhalf] + parts[3][nhalf:]).reshape(partial_value.shape)

    expert_sum = lax.all_to_all(ex_sum, "mdl", split_axis=1, concat_axis=2, tiled=True)
    grad_experts = outer_experts[0] - expert_sum / groups
    grad_dense = outer_dense - dense_sum / groups
    grad_small = outer_small - small_sum / groups
    grad_embed = jnp.dot(
        coefficient, basis_part.T, precision=hi_prec, preferred_element_type=jnp.float32
    )
    expert_outer, expert_moment = nesterov(outer_experts[0], moment_experts[0], grad_experts)
    dense_outer, dense_moment = nesterov(outer_dense, moment_dense, grad_dense)
    small_outer, small_moment = nesterov(outer_small, moment_small, grad_small)
    embed_outer, embed_moment = nesterov(outer_embed, moment_embed, grad_embed)
    spread = lax.all_to_all(
        expert_outer.astype(jnp.bfloat16), "mdl", split_axis=2, concat_axis=1, tiled=True
    )

    pieces = [
        spread,
        dense_outer.astype(jnp.bfloat16),
        small_outer.astype(jnp.bfloat16),
        embed_outer.astype(jnp.bfloat16),
    ]
    flat = jnp.concatenate([p.reshape(-1, lanes) for p in pieces])
    blocks = rep_gather(flat, groups)
    outs = []
    start = 0
    for p in pieces:
        n = p.size // lanes
        g = jnp.stack([b[start : start + n] for b in blocks]).reshape((groups,) + p.shape)
        start += n
        if p.ndim == 3:
            g = g.transpose(1, 0, 2, 3).reshape(p.shape[0], groups * p.shape[1], p.shape[2])
        else:
            g = g.transpose(1, 0, 2).reshape(p.shape[0], groups * p.shape[1])
        outs.append(g)

    return (
        expert_outer[None],
        expert_moment[None],
        outs[0][None],
        dense_outer,
        dense_moment,
        outs[1],
        small_outer,
        small_moment,
        outs[2],
        embed_outer,
        embed_moment,
        outs[3],
    )


def solution(mesh):
    placed = (
        P("rep", "exp", None, None, "mdl"),
        P("rep", ("exp", "mdl"), None),
        P("rep", None, None),
        P("rep", ("exp", "mdl"), None),
        P("exp", None, ("rep", "mdl"), None),
        P(("exp", "mdl"), "rep"),
        P(None, "rep"),
        P(("exp", "mdl"), "rep"),
        P("exp", None, ("rep", "mdl"), None),
        P(("exp", "mdl"), "rep"),
        P(None, "rep"),
        P(("exp", "mdl"), "rep"),
        P(),
    )
    return jax.shard_map(
        on_device,
        mesh=mesh,
        in_specs=placed,
        out_specs=(
            P("exp", None, ("rep", "mdl"), None),
            P("exp", None, ("rep", "mdl"), None),
            P("exp", None, None, "mdl"),
            P(("exp", "mdl"), "rep"),
            P(("exp", "mdl"), "rep"),
            P(("exp", "mdl"), None),
            P(None, "rep"),
            P(None, "rep"),
            P(),
            P(("exp", "mdl"), "rep"),
            P(("exp", "mdl"), "rep"),
            P(("exp", "mdl"), None),
        ),
        check_vma=False,
    )
```

```python
import jax
import jax.numpy as jnp
from jax import lax
from jax.sharding import PartitionSpec as P

decay_rate = 0.5
outer_rate = 0.7


def nesterov(outer, moment, grad_value):
    moment_new = decay_rate * moment + grad_value
    outer_new = outer - outer_rate * (grad_value + decay_rate * moment_new)
    return (outer_new, moment_new)


def split_rows(x, parts):
    rows, cols = x.shape
    return x.reshape(rows, parts, cols // parts).transpose(1, 0, 2).reshape(parts, -1)


def to_next(x, groups):
    return lax.ppermute(x, "rep", [(i, (i + 1) % groups) for i in range(groups)])


def to_prev(x, groups):
    return lax.ppermute(x, "rep", [(i, (i - 1) % groups) for i in range(groups)])


def rep_exchange(send, raw_rows, groups):
    assert groups == 4
    me = lax.axis_index("rep")
    rel = [lax.dynamic_index_in_dim(send, (me + d) % groups, 0, False) for d in range(groups)]
    k = send.shape[1]
    m = k - raw_rows
    h = m // 2
    rh = raw_rows // 2
    f32 = jnp.float32
    bf = send.dtype
    a = to_next(jnp.concatenate([rel[2][:h], rel[2][m : m + rh]]), groups)
    b = to_prev(jnp.concatenate([rel[2][h:m], rel[2][m + rh :]]), groups)
    x = to_next(
        jnp.concatenate(
            [(rel[1][:h].astype(f32) + a[:h].astype(f32)).astype(bf), rel[1][h:], a[h:]]
        ),
        groups,
    )
    y = to_prev(
        jnp.concatenate(
            [rel[3][:h], (rel[3][h:m].astype(f32) + b[: m - h].astype(f32)).astype(bf), rel[3][m:], b[m - h :]]
        ),
        groups,
    )
    near = rel[0].astype(f32) + x[:k].astype(f32) + y[:k].astype(f32)
    far_raw = jnp.concatenate([x[k:], y[k:]]).astype(f32)
    return jnp.concatenate([near[:m], near[m:] + far_raw])


def rep_gather(flat, groups):
    assert groups == 4
    me = lax.axis_index("rep")
    n = flat.shape[0]
    half = n // 2
    from_prev = to_next(flat, groups)
    from_next = to_prev(flat, groups)
    far_a = to_next(from_prev[:half], groups)
    far_b = to_prev(from_next[half:], groups)
    far = jnp.concatenate([far_a, far_b])
    rel = jnp.stack([flat, from_next, far, from_prev])
    return [lax.dynamic_index_in_dim(rel, (j - me) % groups, 0, False) for j in range(groups)]


def on_device(
    inner_experts,
    inner_dense,
    inner_small,
    inner_embed,
    outer_experts,
    outer_dense,
    outer_small,
    outer_embed,
    moment_experts,
    moment_dense,
    moment_small,
    moment_embed,
    embed_basis,
):
    groups = lax.axis_size("rep")
    hi_prec = lax.Precision.HIGHEST
    lanes = 128
    f32 = jnp.float32
    bf = jnp.bfloat16

    own_shard = inner_experts[0, 0]
    halves, all_rows, my_cols = own_shard.shape
    rep_rows = all_rows // groups

    def expert_send(h):
        return own_shard[h].reshape(groups, rep_rows * my_cols // lanes, lanes)

    de_send = split_rows(inner_dense[0], groups).reshape(groups, -1, lanes)
    sm_send = split_rows(inner_small[0], groups).reshape(groups, -1, lanes)
    col_count = outer_embed.shape[1]
    offset = lax.axis_index("rep") * col_count
    basis_part = lax.dynamic_slice_in_dim(embed_basis, offset, col_count, 0)
    partial_value = jnp.dot(
        outer_embed, basis_part, precision=hi_prec, preferred_element_type=f32
    ) - jnp.dot(
        inner_embed[0].astype(f32), embed_basis, precision=hi_prec, preferred_element_type=f32
    ) / groups
    part_hi = partial_value.astype(bf)
    part_lo = (partial_value - part_hi.astype(f32)).astype(bf)
    pp = jnp.concatenate([part_hi.reshape(-1, lanes), part_lo.reshape(-1, lanes)])
    pp_send = jnp.broadcast_to(pp[None], (groups,) + pp.shape)

    ex_rows = rep_rows * my_cols // lanes
    send_a = jnp.concatenate([expert_send(0), de_send, sm_send, pp_send], axis=1)
    send_b = expert_send(1)
    total_a = rep_exchange(send_a, pp.shape[0], groups)
    send_b, total_a = lax.optimization_barrier((send_b, total_a))
    total_b = rep_exchange(send_b, 0, groups)

    sizes = [ex_rows, de_send.shape[1], sm_send.shape[1], pp.shape[0]]
    bounds = [0]
    for n in sizes:
        bounds.append(bounds[-1] + n)
    parts = [total_a[bounds[i] : bounds[i + 1]] for i in range(4)]
    dense_sum = parts[1].reshape(outer_dense.shape)
    small_sum = parts[2].reshape(outer_small.shape)
    nhalf = parts[3].shape[0] // 2
    coefficient = (parts[3][:nhalf] + parts[3][nhalf:]).reshape(partial_value.shape)

    def expert_half(ex_total, h):
        ex_sum = ex_total.reshape(rep_rows, my_cols)
        expert_sum = lax.all_to_all(ex_sum, "mdl", split_axis=0, concat_axis=1, tiled=True)
        grad = outer_experts[0, h] - expert_sum / groups
        e_outer, e_moment = nesterov(outer_experts[0, h], moment_experts[0, h], grad)
        spread = lax.all_to_all(e_outer.astype(bf), "mdl", split_axis=1, concat_axis=0, tiled=True)
        return e_outer, e_moment, spread

    ea_outer, ea_moment, spread_a = expert_half(parts[0], 0)
    eb_outer, eb_moment, spread_b = expert_half(total_b, 1)

    grad_dense = outer_dense - dense_sum / groups
    grad_small = outer_small - small_sum / groups
    grad_embed = jnp.dot(coefficient, basis_part.T, precision=hi_prec, preferred_element_type=f32)
    dense_outer, dense_moment = nesterov(outer_dense, moment_dense, grad_dense)
    small_outer, small_moment = nesterov(outer_small, moment_small, grad_small)
    embed_outer, embed_moment = nesterov(outer_embed, moment_embed, grad_embed)

    pieces_a = [
        spread_a,
        dense_outer.astype(bf),
        small_outer.astype(bf),
        embed_outer.astype(bf),
    ]
    flat_a = jnp.concatenate([p.reshape(-1, lanes) for p in pieces_a])
    flat_a, total_b = lax.optimization_barrier((flat_a, total_b))
    blocks_a = rep_gather(flat_a, groups)
    blocks_b = rep_gather(spread_b.reshape(-1, lanes), groups)

    def assemble(blocks, p, start):
        n = p.size // lanes
        g = jnp.stack([b[start : start + n] for b in blocks]).reshape((groups,) + p.shape)
        return g.transpose(1, 0, 2).reshape(p.shape[0], groups * p.shape[1])

    outs = []
    start = 0
    for p in pieces_a:
        if p is spread_a:
            g = jnp.stack([b[: p.size // lanes] for b in blocks_a]).reshape((groups * p.shape[0], p.shape[1]))
        else:
            g = assemble(blocks_a, p, start)
        start += p.size // lanes
        outs.append(g)
    copy_b = jnp.stack(blocks_b).reshape((groups * spread_b.shape[0], spread_b.shape[1]))
    copy_experts = jnp.stack([outs[0], copy_b])

    expert_outer = jnp.stack([ea_outer, eb_outer])
    expert_moment = jnp.stack([ea_moment, eb_moment])
    return (
        expert_outer[None],
        expert_moment[None],
        copy_experts[None],
        dense_outer,
        dense_moment,
        outs[1],
        small_outer,
        small_moment,
        outs[2],
        embed_outer,
        embed_moment,
        outs[3],
    )


def solution(mesh):
    placed = (
        P("rep", "exp", None, None, "mdl"),
        P("rep", ("exp", "mdl"), None),
        P("rep", None, None),
        P("rep", ("exp", "mdl"), None),
        P("exp", None, ("rep", "mdl"), None),
        P(("exp", "mdl"), "rep"),
        P(None, "rep"),
        P(("exp", "mdl"), "rep"),
        P("exp", None, ("rep", "mdl"), None),
        P(("exp", "mdl"), "rep"),
        P(None, "rep"),
        P(("exp", "mdl"), "rep"),
        P(),
    )
    return jax.shard_map(
        on_device,
        mesh=mesh,
        in_specs=placed,
        out_specs=(
            P("exp", None, ("rep", "mdl"), None),
            P("exp", None, ("rep", "mdl"), None),
            P("exp", None, None, "mdl"),
            P(("exp", "mdl"), "rep"),
            P(("exp", "mdl"), "rep"),
            P(("exp", "mdl"), None),
            P(None, "rep"),
            P(None, "rep"),
            P(),
            P(("exp", "mdl"), "rep"),
            P(("exp", "mdl"), "rep"),
            P(("exp", "mdl"), None),
        ),
        check_vma=False,
    )
```

```python
import jax
import jax.numpy as jnp
from jax import lax
from jax.sharding import PartitionSpec as P

decay_rate = 0.5
outer_rate = 0.7


def nesterov(outer, moment, grad_value):
    moment_new = decay_rate * moment + grad_value
    outer_new = outer - outer_rate * (grad_value + decay_rate * moment_new)
    return (outer_new, moment_new)


def split_rows(x, parts):
    rows, cols = x.shape
    return x.reshape(rows, parts, cols // parts).transpose(1, 0, 2).reshape(parts, -1)


def to_next(x, groups):
    return lax.ppermute(x, "rep", [(i, (i + 1) % groups) for i in range(groups)])


def to_prev(x, groups):
    return lax.ppermute(x, "rep", [(i, (i - 1) % groups) for i in range(groups)])


def rep_exchange(send, raw_rows, groups):
    assert groups == 4
    me = lax.axis_index("rep")
    rel = [lax.dynamic_index_in_dim(send, (me + d) % groups, 0, False) for d in range(groups)]
    k = send.shape[1]
    m = k - raw_rows
    h = m // 2
    rh = raw_rows // 2
    f32 = jnp.float32
    bf = send.dtype
    a = to_next(jnp.concatenate([rel[2][:h], rel[2][m : m + rh]]), groups)
    b = to_prev(jnp.concatenate([rel[2][h:m], rel[2][m + rh :]]), groups)
    x = to_next(
        jnp.concatenate(
            [(rel[1][:h].astype(f32) + a[:h].astype(f32)).astype(bf), rel[1][h:], a[h:]]
        ),
        groups,
    )
    y = to_prev(
        jnp.concatenate(
            [rel[3][:h], (rel[3][h:m].astype(f32) + b[: m - h].astype(f32)).astype(bf), rel[3][m:], b[m - h :]]
        ),
        groups,
    )
    near = rel[0].astype(f32) + x[:k].astype(f32) + y[:k].astype(f32)
    far_raw = jnp.concatenate([x[k:], y[k:]]).astype(f32)
    return jnp.concatenate([near[:m], near[m:] + far_raw])


def rep_gather(flat, groups):
    assert groups == 4
    me = lax.axis_index("rep")
    n = flat.shape[0]
    half = n // 2
    from_prev = to_next(flat, groups)
    from_next = to_prev(flat, groups)
    far_a = to_next(from_prev[:half], groups)
    far_b = to_prev(from_next[half:], groups)
    far = jnp.concatenate([far_a, far_b])
    rel = jnp.stack([flat, from_next, far, from_prev])
    return [lax.dynamic_index_in_dim(rel, (j - me) % groups, 0, False) for j in range(groups)]


def on_device(
    inner_experts,
    inner_dense,
    inner_small,
    inner_embed,
    outer_experts,
    outer_dense,
    outer_small,
    outer_embed,
    moment_experts,
    moment_dense,
    moment_small,
    moment_embed,
    embed_basis,
):
    groups = lax.axis_size("rep")
    hi_prec = lax.Precision.HIGHEST

    lanes = 128
    own_shard = inner_experts[0, 0]
    halves, all_rows, my_cols = own_shard.shape
    rep_rows = all_rows // groups
    ex_send = (
        own_shard.reshape(halves, groups, rep_rows, my_cols)
        .transpose(1, 0, 2, 3)
        .reshape(groups, -1, lanes)
    )
    de_send = split_rows(inner_dense[0], groups).reshape(groups, -1, lanes)
    sm_send = split_rows(inner_small[0], groups).reshape(groups, -1, lanes)

    col_count = outer_embed.shape[1]
    offset = lax.axis_index("rep") * col_count
    basis_part = lax.dynamic_slice_in_dim(embed_basis, offset, col_count, 0)
    partial_value = jnp.dot(
        outer_embed, basis_part, precision=hi_prec, preferred_element_type=jnp.float32
    ) - jnp.dot(
        inner_embed[0].astype(jnp.float32),
        embed_basis,
        precision=hi_prec,
        preferred_element_type=jnp.float32,
    ) / groups
    part_hi = partial_value.astype(jnp.bfloat16)
    part_lo = (partial_value - part_hi.astype(jnp.float32)).astype(jnp.bfloat16)
    pp = jnp.concatenate([part_hi.reshape(-1, lanes), part_lo.reshape(-1, lanes)])
    pp_send = jnp.broadcast_to(pp[None], (groups,) + pp.shape)

    sizes = [ex_send.shape[1], de_send.shape[1], sm_send.shape[1], pp.shape[0]]
    send = jnp.concatenate([ex_send, de_send, sm_send, pp_send], axis=1)
    total = rep_exchange(send, pp.shape[0], groups)
    bounds = [0]
    for s in sizes:
        bounds.append(bounds[-1] + s)
    parts = [total[bounds[i] : bounds[i + 1]] for i in range(4)]

    ex_sum = parts[0].reshape(halves, rep_rows, my_cols)
    dense_sum = parts[1].reshape(outer_dense.shape)
    small_sum = parts[2].reshape(outer_small.shape)
    nhalf = parts[3].shape[0] // 2
    coefficient = (parts[3][:nhalf] + parts[3][nhalf:]).reshape(partial_value.shape)

    expert_sum = lax.all_to_all(
        ex_sum.astype(jnp.bfloat16), "mdl", split_axis=1, concat_axis=2, tiled=True
    ).astype(jnp.float32)
    grad_experts = outer_experts[0] - expert_sum / groups
    grad_dense = outer_dense - dense_sum / groups
    grad_small = outer_small - small_sum / groups
    grad_embed = jnp.dot(
        coefficient, basis_part.T, precision=hi_prec, preferred_element_type=jnp.float32
    )
    expert_outer, expert_moment = nesterov(outer_experts[0], moment_experts[0], grad_experts)
    dense_outer, dense_moment = nesterov(outer_dense, moment_dense, grad_dense)
    small_outer, small_moment = nesterov(outer_small, moment_small, grad_small)
    embed_outer, embed_moment = nesterov(outer_embed, moment_embed, grad_embed)
    spread = lax.all_to_all(
        expert_outer.astype(jnp.bfloat16), "mdl", split_axis=2, concat_axis=1, tiled=True
    )

    pieces = [
        spread,
        dense_outer.astype(jnp.bfloat16),
        small_outer.astype(jnp.bfloat16),
        embed_outer.astype(jnp.bfloat16),
    ]
    flat = jnp.concatenate([p.reshape(-1, lanes) for p in pieces])
    blocks = rep_gather(flat, groups)
    outs = []
    start = 0
    for p in pieces:
        n = p.size // lanes
        g = jnp.stack([b[start : start + n] for b in blocks]).reshape((groups,) + p.shape)
        start += n
        if p.ndim == 3:
            g = g.transpose(1, 0, 2, 3).reshape(p.shape[0], groups * p.shape[1], p.shape[2])
        else:
            g = g.transpose(1, 0, 2).reshape(p.shape[0], groups * p.shape[1])
        outs.append(g)

    return (
        expert_outer[None],
        expert_moment[None],
        outs[0][None],
        dense_outer,
        dense_moment,
        outs[1],
        small_outer,
        small_moment,
        outs[2],
        embed_outer,
        embed_moment,
        outs[3],
    )


def solution(mesh):
    placed = (
        P("rep", "exp", None, None, "mdl"),
        P("rep", ("exp", "mdl"), None),
        P("rep", None, None),
        P("rep", ("exp", "mdl"), None),
        P("exp", None, ("rep", "mdl"), None),
        P(("exp", "mdl"), "rep"),
        P(None, "rep"),
        P(("exp", "mdl"), "rep"),
        P("exp", None, ("rep", "mdl"), None),
        P(("exp", "mdl"), "rep"),
        P(None, "rep"),
        P(("exp", "mdl"), "rep"),
        P(),
    )
    return jax.shard_map(
        on_device,
        mesh=mesh,
        in_specs=placed,
        out_specs=(
            P("exp", None, ("rep", "mdl"), None),
            P("exp", None, ("rep", "mdl"), None),
            P("exp", None, None, "mdl"),
            P(("exp", "mdl"), "rep"),
            P(("exp", "mdl"), "rep"),
            P(("exp", "mdl"), None),
            P(None, "rep"),
            P(None, "rep"),
            P(),
            P(("exp", "mdl"), "rep"),
            P(("exp", "mdl"), "rep"),
            P(("exp", "mdl"), None),
        ),
        check_vma=False,
    )
```

```python
import jax
import jax.numpy as jnp
from jax import lax
from jax.sharding import PartitionSpec as P

decay_rate = 0.5
outer_rate = 0.7


def nesterov(outer, moment, grad_value):
    moment_new = decay_rate * moment + grad_value
    outer_new = outer - outer_rate * (grad_value + decay_rate * moment_new)
    return (outer_new, moment_new)


def split_rows(x, parts):
    rows, cols = x.shape
    return x.reshape(rows, parts, cols // parts).transpose(1, 0, 2).reshape(parts, -1)


def to_next(x, groups):
    return lax.ppermute(x, "rep", [(i, (i + 1) % groups) for i in range(groups)])


def to_prev(x, groups):
    return lax.ppermute(x, "rep", [(i, (i - 1) % groups) for i in range(groups)])


def rep_exchange(send, raw_rows, groups):
    assert groups == 4
    me = lax.axis_index("rep")
    rel = [lax.dynamic_index_in_dim(send, (me + d) % groups, 0, False) for d in range(groups)]
    k = send.shape[1]
    m = k - raw_rows
    h = m // 2
    rh = raw_rows // 2
    f32 = jnp.float32
    bf = send.dtype
    a = to_next(jnp.concatenate([rel[2][:h], rel[2][m : m + rh], rel[1][h:m], rel[1][m:]]), groups)
    b = to_prev(jnp.concatenate([rel[2][h:m], rel[2][m + rh :], rel[3][:h], rel[3][m:]]), groups)
    a_relay, a_pp_relay = a[:h], a[h : h + rh]
    a_near, a_pp = a[h + rh : h + rh + m - h], a[h + rh + m - h :]
    b_relay, b_pp_relay = b[: m - h], b[m - h : m - h + raw_rows - rh]
    b_near, b_pp = b[m - h + raw_rows - rh : m - h + raw_rows - rh + h], b[m - h + raw_rows - rh + h :]
    c = to_next(
        jnp.concatenate([(rel[1][:h].astype(f32) + a_relay.astype(f32)).astype(bf), a_pp_relay]),
        groups,
    )
    d = to_prev(
        jnp.concatenate([(rel[3][h:m].astype(f32) + b_relay.astype(f32)).astype(bf), b_pp_relay]),
        groups,
    )
    first = rel[0][:h].astype(f32) + c[:h].astype(f32) + b_near.astype(f32)
    second = rel[0][h:m].astype(f32) + a_near.astype(f32) + d[: m - h].astype(f32)
    raw = (
        rel[0][m:].astype(f32)
        + a_pp.astype(f32)
        + b_pp.astype(f32)
        + jnp.concatenate([c[h:], d[m - h :]]).astype(f32)
    )
    return jnp.concatenate([first, second, raw])


def rep_gather(flat, groups):
    assert groups == 4
    me = lax.axis_index("rep")
    n = flat.shape[0]
    half = n // 2
    from_prev = to_next(flat, groups)
    from_next = to_prev(flat, groups)
    far_a = to_next(from_prev[:half], groups)
    far_b = to_prev(from_next[half:], groups)
    far = jnp.concatenate([far_a, far_b])
    rel = jnp.stack([flat, from_next, far, from_prev])
    return [lax.dynamic_index_in_dim(rel, (j - me) % groups, 0, False) for j in range(groups)]


def on_device(
    inner_experts,
    inner_dense,
    inner_small,
    inner_embed,
    outer_experts,
    outer_dense,
    outer_small,
    outer_embed,
    moment_experts,
    moment_dense,
    moment_small,
    moment_embed,
    embed_basis,
):
    groups = lax.axis_size("rep")
    hi_prec = lax.Precision.HIGHEST

    lanes = 128
    own_shard = inner_experts[0, 0]
    halves, all_rows, my_cols = own_shard.shape
    rep_rows = all_rows // groups
    ex_send = (
        own_shard.reshape(halves, groups, rep_rows, my_cols)
        .transpose(1, 0, 2, 3)
        .reshape(groups, -1, lanes)
    )
    de_send = split_rows(inner_dense[0], groups).reshape(groups, -1, lanes)
    sm_send = split_rows(inner_small[0], groups).reshape(groups, -1, lanes)

    col_count = outer_embed.shape[1]
    offset = lax.axis_index("rep") * col_count
    basis_part = lax.dynamic_slice_in_dim(embed_basis, offset, col_count, 0)
    partial_value = jnp.dot(
        outer_embed, basis_part, precision=hi_prec, preferred_element_type=jnp.float32
    ) - jnp.dot(
        inner_embed[0].astype(jnp.float32),
        embed_basis,
        precision=hi_prec,
        preferred_element_type=jnp.float32,
    ) / groups
    part_hi = partial_value.astype(jnp.bfloat16)
    part_lo = (partial_value - part_hi.astype(jnp.float32)).astype(jnp.bfloat16)
    pp = jnp.concatenate([part_hi.reshape(-1, lanes), part_lo.reshape(-1, lanes)])
    pp_send = jnp.broadcast_to(pp[None], (groups,) + pp.shape)

    sizes = [ex_send.shape[1], de_send.shape[1], sm_send.shape[1], pp.shape[0]]
    send = jnp.concatenate([ex_send, de_send, sm_send, pp_send], axis=1)
    total = rep_exchange(send, pp.shape[0], groups)
    bounds = [0]
    for s in sizes:
        bounds.append(bounds[-1] + s)
    parts = [total[bounds[i] : bounds[i + 1]] for i in range(4)]

    ex_sum = parts[0].reshape(halves, rep_rows, my_cols)
    dense_sum = parts[1].reshape(outer_dense.shape)
    small_sum = parts[2].reshape(outer_small.shape)
    nhalf = parts[3].shape[0] // 2
    coefficient = (parts[3][:nhalf] + parts[3][nhalf:]).reshape(partial_value.shape)

    expert_sum = lax.all_to_all(
        ex_sum.astype(jnp.bfloat16), "mdl", split_axis=1, concat_axis=2, tiled=True
    ).astype(jnp.float32)
    grad_experts = outer_experts[0] - expert_sum / groups
    grad_dense = outer_dense - dense_sum / groups
    grad_small = outer_small - small_sum / groups
    grad_embed = jnp.dot(
        coefficient, basis_part.T, precision=hi_prec, preferred_element_type=jnp.float32
    )
    expert_outer, expert_moment = nesterov(outer_experts[0], moment_experts[0], grad_experts)
    dense_outer, dense_moment = nesterov(outer_dense, moment_dense, grad_dense)
    small_outer, small_moment = nesterov(outer_small, moment_small, grad_small)
    embed_outer, embed_moment = nesterov(outer_embed, moment_embed, grad_embed)
    spread = lax.all_to_all(
        expert_outer.astype(jnp.bfloat16), "mdl", split_axis=2, concat_axis=1, tiled=True
    )

    pieces = [
        spread,
        dense_outer.astype(jnp.bfloat16),
        small_outer.astype(jnp.bfloat16),
        embed_outer.astype(jnp.bfloat16),
    ]
    flat = jnp.concatenate([p.reshape(-1, lanes) for p in pieces])
    blocks = rep_gather(flat, groups)
    outs = []
    start = 0
    for p in pieces:
        n = p.size // lanes
        g = jnp.stack([b[start : start + n] for b in blocks]).reshape((groups,) + p.shape)
        start += n
        if p.ndim == 3:
            g = g.transpose(1, 0, 2, 3).reshape(p.shape[0], groups * p.shape[1], p.shape[2])
        else:
            g = g.transpose(1, 0, 2).reshape(p.shape[0], groups * p.shape[1])
        outs.append(g)

    return (
        expert_outer[None],
        expert_moment[None],
        outs[0][None],
        dense_outer,
        dense_moment,
        outs[1],
        small_outer,
        small_moment,
        outs[2],
        embed_outer,
        embed_moment,
        outs[3],
    )


def solution(mesh):
    placed = (
        P("rep", "exp", None, None, "mdl"),
        P("rep", ("exp", "mdl"), None),
        P("rep", None, None),
        P("rep", ("exp", "mdl"), None),
        P("exp", None, ("rep", "mdl"), None),
        P(("exp", "mdl"), "rep"),
        P(None, "rep"),
        P(("exp", "mdl"), "rep"),
        P("exp", None, ("rep", "mdl"), None),
        P(("exp", "mdl"), "rep"),
        P(None, "rep"),
        P(("exp", "mdl"), "rep"),
        P(),
    )
    return jax.shard_map(
        on_device,
        mesh=mesh,
        in_specs=placed,
        out_specs=(
            P("exp", None, ("rep", "mdl"), None),
            P("exp", None, ("rep", "mdl"), None),
            P("exp", None, None, "mdl"),
            P(("exp", "mdl"), "rep"),
            P(("exp", "mdl"), "rep"),
            P(("exp", "mdl"), None),
            P(None, "rep"),
            P(None, "rep"),
            P(),
            P(("exp", "mdl"), "rep"),
            P(("exp", "mdl"), "rep"),
            P(("exp", "mdl"), None),
        ),
        check_vma=False,
    )
```

```python
import jax
import jax.numpy as jnp
from jax import lax
from jax.sharding import PartitionSpec as P

decay_rate = 0.5
outer_rate = 0.7


def nesterov(outer, moment, grad_value):
    moment_new = decay_rate * moment + grad_value
    outer_new = outer - outer_rate * (grad_value + decay_rate * moment_new)
    return (outer_new, moment_new)


def split_rows(x, parts):
    rows, cols = x.shape
    return x.reshape(rows, parts, cols // parts).transpose(1, 0, 2).reshape(parts, -1)


def to_next(x, groups):
    return lax.ppermute(x, "rep", [(i, (i + 1) % groups) for i in range(groups)])


def to_prev(x, groups):
    return lax.ppermute(x, "rep", [(i, (i - 1) % groups) for i in range(groups)])


def rep_exchange(send, raw_rows, groups):
    assert groups == 4
    me = lax.axis_index("rep")
    rel = [lax.dynamic_index_in_dim(send, (me + d) % groups, 0, False) for d in range(groups)]
    k = send.shape[1]
    m = k - raw_rows
    h = m // 2
    rh = raw_rows // 2
    f32 = jnp.float32
    bf = send.dtype
    a = to_next(jnp.concatenate([rel[2][:h], rel[2][m : m + rh], rel[1][h:m], rel[1][m:]]), groups)
    b = to_prev(jnp.concatenate([rel[2][h:m], rel[2][m + rh :], rel[3][:h], rel[3][m:]]), groups)
    a_relay, a_pp_relay = a[:h], a[h : h + rh]
    a_near, a_pp = a[h + rh : h + rh + m - h], a[h + rh + m - h :]
    b_relay, b_pp_relay = b[: m - h], b[m - h : m - h + raw_rows - rh]
    b_near, b_pp = b[m - h + raw_rows - rh : m - h + raw_rows - rh + h], b[m - h + raw_rows - rh + h :]
    c = to_next(
        jnp.concatenate([(rel[1][:h].astype(f32) + a_relay.astype(f32)).astype(bf), a_pp_relay]),
        groups,
    )
    d = to_prev(
        jnp.concatenate([(rel[3][h:m].astype(f32) + b_relay.astype(f32)).astype(bf), b_pp_relay]),
        groups,
    )
    first = rel[0][:h].astype(f32) + c[:h].astype(f32) + b_near.astype(f32)
    second = rel[0][h:m].astype(f32) + a_near.astype(f32) + d[: m - h].astype(f32)
    raw = (
        rel[0][m:].astype(f32)
        + a_pp.astype(f32)
        + b_pp.astype(f32)
        + jnp.concatenate([c[h:], d[m - h :]]).astype(f32)
    )
    return jnp.concatenate([first, second, raw])


def rep_gather(flat, groups):
    assert groups == 4
    me = lax.axis_index("rep")
    n = flat.shape[0]
    half = n // 2
    from_prev = to_next(flat, groups)
    from_next = to_prev(flat, groups)
    far_a = to_next(from_prev[:half], groups)
    far_b = to_prev(from_next[half:], groups)
    far = jnp.concatenate([far_a, far_b])
    rel = jnp.stack([flat, from_next, far, from_prev])
    return [lax.dynamic_index_in_dim(rel, (j - me) % groups, 0, False) for j in range(groups)]


def on_device(
    inner_experts,
    inner_dense,
    inner_small,
    inner_embed,
    outer_experts,
    outer_dense,
    outer_small,
    outer_embed,
    moment_experts,
    moment_dense,
    moment_small,
    moment_embed,
    embed_basis,
):
    groups = lax.axis_size("rep")
    hi_prec = lax.Precision.HIGHEST

    lanes = 128
    own_shard = inner_experts[0, 0]
    halves, all_rows, my_cols = own_shard.shape
    rep_rows = all_rows // groups
    mdl_size = lax.axis_size("mdl")
    own_rows = rep_rows // mdl_size
    ex_send = (
        own_shard.reshape(halves, groups, mdl_size, own_rows, my_cols)
        .transpose(1, 2, 0, 3, 4)
        .reshape(groups, -1, lanes)
    )
    de_send = split_rows(inner_dense[0], groups).reshape(groups, -1, lanes)
    sm_send = split_rows(inner_small[0], groups).reshape(groups, -1, lanes)

    col_count = outer_embed.shape[1]
    offset = lax.axis_index("rep") * col_count
    basis_part = lax.dynamic_slice_in_dim(embed_basis, offset, col_count, 0)
    partial_value = jnp.dot(
        outer_embed, basis_part, precision=hi_prec, preferred_element_type=jnp.float32
    ) - jnp.dot(
        inner_embed[0].astype(jnp.float32),
        embed_basis,
        precision=hi_prec,
        preferred_element_type=jnp.float32,
    ) / groups
    part_hi = partial_value.astype(jnp.bfloat16)
    part_lo = (partial_value - part_hi.astype(jnp.float32)).astype(jnp.bfloat16)
    pp = jnp.concatenate([part_hi.reshape(-1, lanes), part_lo.reshape(-1, lanes)])
    pp_send = jnp.broadcast_to(pp[None], (groups,) + pp.shape)

    sizes = [ex_send.shape[1], de_send.shape[1], sm_send.shape[1], pp.shape[0]]
    send = jnp.concatenate([ex_send, de_send, sm_send, pp_send], axis=1)
    total = rep_exchange(send, pp.shape[0], groups)
    bounds = [0]
    for s in sizes:
        bounds.append(bounds[-1] + s)
    parts = [total[bounds[i] : bounds[i + 1]] for i in range(4)]

    ex_sum = parts[0].reshape(mdl_size, halves, own_rows, my_cols)
    dense_sum = parts[1].reshape(outer_dense.shape)
    small_sum = parts[2].reshape(outer_small.shape)
    nhalf = parts[3].shape[0] // 2
    coefficient = (parts[3][:nhalf] + parts[3][nhalf:]).reshape(partial_value.shape)

    expert_sum = lax.all_to_all(
        ex_sum.astype(jnp.bfloat16), "mdl", split_axis=0, concat_axis=0, tiled=True
    ).astype(jnp.float32)
    expert_sum = expert_sum.transpose(1, 2, 0, 3).reshape(outer_experts.shape[1:])
    grad_experts = outer_experts[0] - expert_sum / groups
    grad_dense = outer_dense - dense_sum / groups
    grad_small = outer_small - small_sum / groups
    grad_embed = jnp.dot(
        coefficient, basis_part.T, precision=hi_prec, preferred_element_type=jnp.float32
    )
    expert_outer, expert_moment = nesterov(outer_experts[0], moment_experts[0], grad_experts)
    dense_outer, dense_moment = nesterov(outer_dense, moment_dense, grad_dense)
    small_outer, small_moment = nesterov(outer_small, moment_small, grad_small)
    embed_outer, embed_moment = nesterov(outer_embed, moment_embed, grad_embed)
    spread = lax.all_to_all(
        expert_outer.astype(jnp.bfloat16)
        .reshape(halves, own_rows, mdl_size, my_cols)
        .transpose(2, 0, 1, 3),
        "mdl",
        split_axis=0,
        concat_axis=0,
        tiled=True,
    )

    pieces = [
        spread,
        dense_outer.astype(jnp.bfloat16),
        small_outer.astype(jnp.bfloat16),
        embed_outer.astype(jnp.bfloat16),
    ]
    flat = jnp.concatenate([p.reshape(-1, lanes) for p in pieces])
    blocks = rep_gather(flat, groups)
    outs = []
    start = 0
    for p in pieces:
        n = p.size // lanes
        g = jnp.stack([b[start : start + n] for b in blocks]).reshape((groups,) + p.shape)
        start += n
        if p.ndim == 4:
            g = g.transpose(2, 0, 1, 3, 4).reshape(halves, all_rows, my_cols)
        else:
            g = g.transpose(1, 0, 2).reshape(p.shape[0], groups * p.shape[1])
        outs.append(g)

    return (
        expert_outer[None],
        expert_moment[None],
        outs[0][None],
        dense_outer,
        dense_moment,
        outs[1],
        small_outer,
        small_moment,
        outs[2],
        embed_outer,
        embed_moment,
        outs[3],
    )


def solution(mesh):
    placed = (
        P("rep", "exp", None, None, "mdl"),
        P("rep", ("exp", "mdl"), None),
        P("rep", None, None),
        P("rep", ("exp", "mdl"), None),
        P("exp", None, ("rep", "mdl"), None),
        P(("exp", "mdl"), "rep"),
        P(None, "rep"),
        P(("exp", "mdl"), "rep"),
        P("exp", None, ("rep", "mdl"), None),
        P(("exp", "mdl"), "rep"),
        P(None, "rep"),
        P(("exp", "mdl"), "rep"),
        P(),
    )
    return jax.shard_map(
        on_device,
        mesh=mesh,
        in_specs=placed,
        out_specs=(
            P("exp", None, ("rep", "mdl"), None),
            P("exp", None, ("rep", "mdl"), None),
            P("exp", None, None, "mdl"),
            P(("exp", "mdl"), "rep"),
            P(("exp", "mdl"), "rep"),
            P(("exp", "mdl"), None),
            P(None, "rep"),
            P(None, "rep"),
            P(),
            P(("exp", "mdl"), "rep"),
            P(("exp", "mdl"), "rep"),
            P(("exp", "mdl"), None),
        ),
        check_vma=False,
    )
```

```python
import jax
import jax.numpy as jnp
from jax import lax
from jax.sharding import PartitionSpec as P

decay_rate = 0.5
outer_rate = 0.7


def nesterov(outer, moment, grad_value):
    moment_new = decay_rate * moment + grad_value
    outer_new = outer - outer_rate * (grad_value + decay_rate * moment_new)
    return (outer_new, moment_new)


def split_rows(x, parts):
    rows, cols = x.shape
    return x.reshape(rows, parts, cols // parts).transpose(1, 0, 2).reshape(parts, -1)


def to_next(x, groups):
    return lax.ppermute(x, "rep", [(i, (i + 1) % groups) for i in range(groups)])


def to_prev(x, groups):
    return lax.ppermute(x, "rep", [(i, (i - 1) % groups) for i in range(groups)])


def rep_exchange(send, raw_rows, groups):
    assert groups == 4
    me = lax.axis_index("rep")
    rel = [lax.dynamic_index_in_dim(send, (me + d) % groups, 0, False) for d in range(groups)]
    k = send.shape[1]
    m = k - raw_rows
    h = m // 2
    rh = raw_rows // 2
    f32 = jnp.float32
    bf = send.dtype
    a = to_next(jnp.concatenate([rel[2][:h], rel[2][m : m + rh], rel[1][h:m], rel[1][m:]]), groups)
    b = to_prev(jnp.concatenate([rel[2][h:m], rel[2][m + rh :], rel[3][:h], rel[3][m:]]), groups)
    a_relay, a_pp_relay = a[:h], a[h : h + rh]
    a_near, a_pp = a[h + rh : h + rh + m - h], a[h + rh + m - h :]
    b_relay, b_pp_relay = b[: m - h], b[m - h : m - h + raw_rows - rh]
    b_near, b_pp = b[m - h + raw_rows - rh : m - h + raw_rows - rh + h], b[m - h + raw_rows - rh + h :]
    c = to_next(
        jnp.concatenate([(rel[1][:h].astype(f32) + a_relay.astype(f32)).astype(bf), a_pp_relay]),
        groups,
    )
    d = to_prev(
        jnp.concatenate([(rel[3][h:m].astype(f32) + b_relay.astype(f32)).astype(bf), b_pp_relay]),
        groups,
    )
    first = rel[0][:h].astype(f32) + c[:h].astype(f32) + b_near.astype(f32)
    second = rel[0][h:m].astype(f32) + a_near.astype(f32) + d[: m - h].astype(f32)
    raw = (
        rel[0][m:].astype(f32)
        + a_pp.astype(f32)
        + b_pp.astype(f32)
        + jnp.concatenate([c[h:], d[m - h :]]).astype(f32)
    )
    return jnp.concatenate([first, second, raw])


def rep_gather(flat, groups):
    assert groups == 4
    me = lax.axis_index("rep")
    n = flat.shape[0]
    half = n // 2
    from_prev = to_next(flat, groups)
    from_next = to_prev(flat, groups)
    far_a = to_next(from_prev[:half], groups)
    far_b = to_prev(from_next[half:], groups)
    far = jnp.concatenate([far_a, far_b])
    rel = jnp.stack([flat, from_next, far, from_prev])
    return [lax.dynamic_index_in_dim(rel, (j - me) % groups, 0, False) for j in range(groups)]


def on_device(
    inner_experts,
    inner_dense,
    inner_small,
    inner_embed,
    outer_experts,
    outer_dense,
    outer_small,
    outer_embed,
    moment_experts,
    moment_dense,
    moment_small,
    moment_embed,
    embed_basis,
):
    groups = lax.axis_size("rep")
    hi_prec = lax.Precision.HIGHEST

    lanes = 128
    own_shard = inner_experts[0, 0]
    halves, all_rows, my_cols = own_shard.shape
    rep_rows = all_rows // groups
    mdl_size = lax.axis_size("mdl")
    own_rows = rep_rows // mdl_size
    ex_send = (
        own_shard.reshape(halves, groups, mdl_size, own_rows, my_cols)
        .transpose(1, 2, 0, 3, 4)
        .reshape(groups, -1, lanes)
    )
    de_send = split_rows(inner_dense[0], groups).reshape(groups, -1, lanes)
    sm_send = split_rows(inner_small[0], groups).reshape(groups, -1, lanes)

    col_count = outer_embed.shape[1]
    offset = lax.axis_index("rep") * col_count
    basis_part = lax.dynamic_slice_in_dim(embed_basis, offset, col_count, 0)
    partial_value = jnp.dot(
        jnp.concatenate([outer_embed, inner_embed[0].astype(jnp.float32) / groups], axis=1),
        jnp.concatenate([basis_part, -embed_basis], axis=0),
        precision=hi_prec,
        preferred_element_type=jnp.float32,
    )
    part_hi = partial_value.astype(jnp.bfloat16)
    part_lo = (partial_value - part_hi.astype(jnp.float32)).astype(jnp.bfloat16)
    pp = jnp.concatenate([part_hi.reshape(-1, lanes), part_lo.reshape(-1, lanes)])
    pp_send = jnp.broadcast_to(pp[None], (groups,) + pp.shape)

    sizes = [ex_send.shape[1], de_send.shape[1], sm_send.shape[1], pp.shape[0]]
    send = jnp.concatenate([ex_send, de_send, sm_send, pp_send], axis=1)
    total = rep_exchange(send, pp.shape[0], groups)
    bounds = [0]
    for s in sizes:
        bounds.append(bounds[-1] + s)
    parts = [total[bounds[i] : bounds[i + 1]] for i in range(4)]

    ex_sum = parts[0].reshape(mdl_size, halves, own_rows, my_cols)
    dense_sum = parts[1].reshape(outer_dense.shape)
    small_sum = parts[2].reshape(outer_small.shape)
    nhalf = parts[3].shape[0] // 2
    coefficient = (parts[3][:nhalf] + parts[3][nhalf:]).reshape(partial_value.shape)

    expert_sum = lax.all_to_all(
        ex_sum.astype(jnp.bfloat16), "mdl", split_axis=0, concat_axis=0, tiled=True
    ).astype(jnp.float32)
    expert_sum = expert_sum.transpose(1, 2, 0, 3).reshape(outer_experts.shape[1:])
    grad_experts = outer_experts[0] - expert_sum / groups
    grad_dense = outer_dense - dense_sum / groups
    grad_small = outer_small - small_sum / groups
    grad_embed = jnp.dot(
        coefficient, basis_part.T, precision=hi_prec, preferred_element_type=jnp.float32
    )
    expert_outer, expert_moment = nesterov(outer_experts[0], moment_experts[0], grad_experts)
    dense_outer, dense_moment = nesterov(outer_dense, moment_dense, grad_dense)
    small_outer, small_moment = nesterov(outer_small, moment_small, grad_small)
    embed_outer, embed_moment = nesterov(outer_embed, moment_embed, grad_embed)
    spread = lax.all_to_all(
        expert_outer.astype(jnp.bfloat16)
        .reshape(halves, own_rows, mdl_size, my_cols)
        .transpose(2, 0, 1, 3),
        "mdl",
        split_axis=0,
        concat_axis=0,
        tiled=True,
    )

    pieces = [
        spread,
        dense_outer.astype(jnp.bfloat16),
        small_outer.astype(jnp.bfloat16),
        embed_outer.astype(jnp.bfloat16),
    ]
    flat = jnp.concatenate([p.reshape(-1, lanes) for p in pieces])
    blocks = rep_gather(flat, groups)
    outs = []
    start = 0
    for p in pieces:
        n = p.size // lanes
        g = [b[start : start + n].reshape(p.shape) for b in blocks]
        start += n
        if p.ndim == 4:
            g = jnp.concatenate(
                [x.transpose(1, 0, 2, 3).reshape(halves, rep_rows, my_cols) for x in g], axis=1
            )
        else:
            g = jnp.concatenate(g, axis=1)
        outs.append(g)

    return (
        expert_outer[None],
        expert_moment[None],
        outs[0][None],
        dense_outer,
        dense_moment,
        outs[1],
        small_outer,
        small_moment,
        outs[2],
        embed_outer,
        embed_moment,
        outs[3],
    )


def solution(mesh):
    placed = (
        P("rep", "exp", None, None, "mdl"),
        P("rep", ("exp", "mdl"), None),
        P("rep", None, None),
        P("rep", ("exp", "mdl"), None),
        P("exp", None, ("rep", "mdl"), None),
        P(("exp", "mdl"), "rep"),
        P(None, "rep"),
        P(("exp", "mdl"), "rep"),
        P("exp", None, ("rep", "mdl"), None),
        P(("exp", "mdl"), "rep"),
        P(None, "rep"),
        P(("exp", "mdl"), "rep"),
        P(),
    )
    return jax.shard_map(
        on_device,
        mesh=mesh,
        in_specs=placed,
        out_specs=(
            P("exp", None, ("rep", "mdl"), None),
            P("exp", None, ("rep", "mdl"), None),
            P("exp", None, None, "mdl"),
            P(("exp", "mdl"), "rep"),
            P(("exp", "mdl"), "rep"),
            P(("exp", "mdl"), None),
            P(None, "rep"),
            P(None, "rep"),
            P(),
            P(("exp", "mdl"), "rep"),
            P(("exp", "mdl"), "rep"),
            P(("exp", "mdl"), None),
        ),
        check_vma=False,
    )
```

```python
import jax
import jax.numpy as jnp
from jax import lax
from jax.sharding import PartitionSpec as P

decay_rate = 0.5
outer_rate = 0.7


def nesterov(outer, moment, grad_value):
    moment_new = decay_rate * moment + grad_value
    outer_new = outer - outer_rate * (grad_value + decay_rate * moment_new)
    return (outer_new, moment_new)


def split_rows(x, parts):
    rows, cols = x.shape
    return x.reshape(rows, parts, cols // parts).transpose(1, 0, 2).reshape(parts, -1)


def to_next(x, groups):
    return lax.ppermute(x, "rep", [(i, (i + 1) % groups) for i in range(groups)])


def to_prev(x, groups):
    return lax.ppermute(x, "rep", [(i, (i - 1) % groups) for i in range(groups)])


def rep_exchange(send, raw_rows, groups):
    assert groups == 4
    me = lax.axis_index("rep")
    rel = [lax.dynamic_index_in_dim(send, (me + d) % groups, 0, False) for d in range(groups)]
    k = send.shape[1]
    m = k - raw_rows
    h = m // 2
    rh = raw_rows // 2
    f32 = jnp.float32
    bf = send.dtype
    a = to_next(jnp.concatenate([rel[2][:h], rel[2][m : m + rh], rel[1][h:m], rel[1][m:]]), groups)
    b = to_prev(jnp.concatenate([rel[2][h:m], rel[2][m + rh :], rel[3][:h], rel[3][m:]]), groups)
    a_relay, a_pp_relay = a[:h], a[h : h + rh]
    a_near, a_pp = a[h + rh : h + rh + m - h], a[h + rh + m - h :]
    b_relay, b_pp_relay = b[: m - h], b[m - h : m - h + raw_rows - rh]
    b_near, b_pp = b[m - h + raw_rows - rh : m - h + raw_rows - rh + h], b[m - h + raw_rows - rh + h :]
    c = to_next(
        jnp.concatenate([(rel[1][:h].astype(f32) + a_relay.astype(f32)).astype(bf), a_pp_relay]),
        groups,
    )
    d = to_prev(
        jnp.concatenate([(rel[3][h:m].astype(f32) + b_relay.astype(f32)).astype(bf), b_pp_relay]),
        groups,
    )
    first = rel[0][:h].astype(f32) + c[:h].astype(f32) + b_near.astype(f32)
    second = rel[0][h:m].astype(f32) + a_near.astype(f32) + d[: m - h].astype(f32)
    raw = (
        rel[0][m:].astype(f32)
        + a_pp.astype(f32)
        + b_pp.astype(f32)
        + jnp.concatenate([c[h:], d[m - h :]]).astype(f32)
    )
    return jnp.concatenate([first, second, raw])


def rep_gather(flat, groups):
    assert groups == 4
    me = lax.axis_index("rep")
    n = flat.shape[0]
    half = n // 2
    from_prev = to_next(flat, groups)
    from_next = to_prev(flat, groups)
    far_a = to_next(from_prev[:half], groups)
    far_b = to_prev(from_next[half:], groups)
    far = jnp.concatenate([far_a, far_b])
    rel = jnp.stack([flat, from_next, far, from_prev])
    return [lax.dynamic_index_in_dim(rel, (j - me) % groups, 0, False) for j in range(groups)]


def on_device(
    inner_experts,
    inner_dense,
    inner_small,
    inner_embed,
    outer_experts,
    outer_dense,
    outer_small,
    outer_embed,
    moment_experts,
    moment_dense,
    moment_small,
    moment_embed,
    embed_basis,
):
    groups = lax.axis_size("rep")
    hi_prec = lax.Precision.HIGHEST

    lanes = 128
    own_shard = inner_experts[0, 0]
    halves, all_rows, my_cols = own_shard.shape
    rep_rows = all_rows // groups
    mdl_size = lax.axis_size("mdl")
    own_rows = rep_rows // mdl_size
    ex_send = (
        own_shard.reshape(halves, groups, mdl_size, own_rows, my_cols)
        .transpose(1, 2, 0, 3, 4)
        .reshape(groups, -1, lanes)
    )
    de_send = split_rows(inner_dense[0], groups).reshape(groups, -1, lanes)
    sm_send = split_rows(inner_small[0], groups).reshape(groups, -1, lanes)

    col_count = outer_embed.shape[1]
    offset = lax.axis_index("rep") * col_count
    basis_part = lax.dynamic_slice_in_dim(embed_basis, offset, col_count, 0)
    partial_value = jnp.dot(
        jnp.concatenate([outer_embed, inner_embed[0].astype(jnp.float32) * (-1.0 / groups)], axis=1),
        jnp.concatenate([basis_part, embed_basis], axis=0),
        precision=hi_prec,
        preferred_element_type=jnp.float32,
    )
    part_hi = partial_value.astype(jnp.bfloat16)
    part_lo = (partial_value - part_hi.astype(jnp.float32)).astype(jnp.bfloat16)
    pp = jnp.concatenate([part_hi.reshape(-1, lanes), part_lo.reshape(-1, lanes)])
    pp_send = jnp.broadcast_to(pp[None], (groups,) + pp.shape)

    sizes = [ex_send.shape[1], de_send.shape[1], sm_send.shape[1], pp.shape[0]]
    send = jnp.concatenate([ex_send, de_send, sm_send, pp_send], axis=1)
    total = rep_exchange(send, pp.shape[0], groups)
    bounds = [0]
    for s in sizes:
        bounds.append(bounds[-1] + s)
    parts = [total[bounds[i] : bounds[i + 1]] for i in range(4)]

    ex_sum = parts[0].reshape(mdl_size, halves, own_rows, my_cols)
    dense_sum = parts[1].reshape(outer_dense.shape)
    small_sum = parts[2].reshape(outer_small.shape)
    nhalf = parts[3].shape[0] // 2
    coefficient = (parts[3][:nhalf] + parts[3][nhalf:]).reshape(partial_value.shape)

    expert_sum = lax.all_to_all(
        ex_sum.astype(jnp.bfloat16), "mdl", split_axis=0, concat_axis=0, tiled=True
    ).astype(jnp.float32)
    expert_sum = expert_sum.transpose(1, 2, 0, 3).reshape(outer_experts.shape[1:])
    grad_experts = outer_experts[0] - expert_sum / groups
    grad_dense = outer_dense - dense_sum / groups
    grad_small = outer_small - small_sum / groups
    grad_embed = jnp.dot(
        coefficient, basis_part.T, precision=hi_prec, preferred_element_type=jnp.float32
    )
    expert_outer, expert_moment = nesterov(outer_experts[0], moment_experts[0], grad_experts)
    dense_outer, dense_moment = nesterov(outer_dense, moment_dense, grad_dense)
    small_outer, small_moment = nesterov(outer_small, moment_small, grad_small)
    embed_outer, embed_moment = nesterov(outer_embed, moment_embed, grad_embed)
    spread = lax.all_to_all(
        expert_outer.astype(jnp.bfloat16)
        .reshape(halves, own_rows, mdl_size, my_cols)
        .transpose(2, 0, 1, 3),
        "mdl",
        split_axis=0,
        concat_axis=0,
        tiled=True,
    )

    pieces = [
        spread,
        dense_outer.astype(jnp.bfloat16),
        small_outer.astype(jnp.bfloat16),
        embed_outer.astype(jnp.bfloat16),
    ]
    flat = jnp.concatenate([p.reshape(-1, lanes) for p in pieces])
    blocks = rep_gather(flat, groups)
    outs = []
    start = 0
    for p in pieces:
        n = p.size // lanes
        g = [b[start : start + n].reshape(p.shape) for b in blocks]
        start += n
        if p.ndim == 4:
            g = jnp.concatenate(
                [x.transpose(1, 0, 2, 3).reshape(halves, rep_rows, my_cols) for x in g], axis=1
            )
        else:
            g = jnp.concatenate(g, axis=1)
        outs.append(g)

    return (
        expert_outer[None],
        expert_moment[None],
        outs[0][None],
        dense_outer,
        dense_moment,
        outs[1],
        small_outer,
        small_moment,
        outs[2],
        embed_outer,
        embed_moment,
        outs[3],
    )


def solution(mesh):
    placed = (
        P("rep", "exp", None, None, "mdl"),
        P("rep", ("exp", "mdl"), None),
        P("rep", None, None),
        P("rep", ("exp", "mdl"), None),
        P("exp", None, ("rep", "mdl"), None),
        P(("exp", "mdl"), "rep"),
        P(None, "rep"),
        P(("exp", "mdl"), "rep"),
        P("exp", None, ("rep", "mdl"), None),
        P(("exp", "mdl"), "rep"),
        P(None, "rep"),
        P(("exp", "mdl"), "rep"),
        P(),
    )
    return jax.shard_map(
        on_device,
        mesh=mesh,
        in_specs=placed,
        out_specs=(
            P("exp", None, ("rep", "mdl"), None),
            P("exp", None, ("rep", "mdl"), None),
            P("exp", None, None, "mdl"),
            P(("exp", "mdl"), "rep"),
            P(("exp", "mdl"), "rep"),
            P(("exp", "mdl"), None),
            P(None, "rep"),
            P(None, "rep"),
            P(),
            P(("exp", "mdl"), "rep"),
            P(("exp", "mdl"), "rep"),
            P(("exp", "mdl"), None),
        ),
        check_vma=False,
    )
```

```python
import jax
import jax.numpy as jnp
from jax import lax
from jax.sharding import PartitionSpec as P

decay_rate = 0.5
outer_rate = 0.7


def nesterov(outer, moment, grad_value):
    moment_new = decay_rate * moment + grad_value
    outer_new = outer - outer_rate * (grad_value + decay_rate * moment_new)
    return (outer_new, moment_new)


def split_rows(x, parts):
    rows, cols = x.shape
    return x.reshape(rows, parts, cols // parts).transpose(1, 0, 2).reshape(parts, -1)


def to_next(x, groups):
    return lax.ppermute(x, "rep", [(i, (i + 1) % groups) for i in range(groups)])


def to_prev(x, groups):
    return lax.ppermute(x, "rep", [(i, (i - 1) % groups) for i in range(groups)])


def rep_exchange(send, raw_rows, groups):
    assert groups == 4
    me = lax.axis_index("rep")
    rel = [lax.dynamic_index_in_dim(send, (me + d) % groups, 0, False) for d in range(groups)]
    k = send.shape[1]
    m = k - raw_rows
    h = m // 2
    rh = raw_rows // 2
    f32 = jnp.float32
    bf = send.dtype
    a = to_next(jnp.concatenate([rel[2][:h], rel[2][m : m + rh], rel[1][h:m], rel[1][m:]]), groups)
    b = to_prev(jnp.concatenate([rel[2][h:m], rel[2][m + rh :], rel[3][:h], rel[3][m:]]), groups)
    a_relay, a_pp_relay = a[:h], a[h : h + rh]
    a_near, a_pp = a[h + rh : h + rh + m - h], a[h + rh + m - h :]
    b_relay, b_pp_relay = b[: m - h], b[m - h : m - h + raw_rows - rh]
    b_near, b_pp = b[m - h + raw_rows - rh : m - h + raw_rows - rh + h], b[m - h + raw_rows - rh + h :]
    c = to_next(
        jnp.concatenate([(rel[1][:h].astype(f32) + a_relay.astype(f32)).astype(bf), a_pp_relay]),
        groups,
    )
    d = to_prev(
        jnp.concatenate([(rel[3][h:m].astype(f32) + b_relay.astype(f32)).astype(bf), b_pp_relay]),
        groups,
    )
    first = rel[0][:h].astype(f32) + c[:h].astype(f32) + b_near.astype(f32)
    second = rel[0][h:m].astype(f32) + a_near.astype(f32) + d[: m - h].astype(f32)
    raw = (
        rel[0][m:].astype(f32)
        + a_pp.astype(f32)
        + b_pp.astype(f32)
        + jnp.concatenate([c[h:], d[m - h :]]).astype(f32)
    )
    return first, second, raw


def rep_gather(flat, groups):
    assert groups == 4
    me = lax.axis_index("rep")
    n = flat.shape[0]
    half = n // 2
    from_prev = to_next(flat, groups)
    from_next = to_prev(flat, groups)
    far_a = to_next(from_prev[:half], groups)
    far_b = to_prev(from_next[half:], groups)
    far = jnp.concatenate([far_a, far_b])
    rel = jnp.stack([flat, from_next, far, from_prev])
    return [lax.dynamic_index_in_dim(rel, (j - me) % groups, 0, False) for j in range(groups)]


def on_device(
    inner_experts,
    inner_dense,
    inner_small,
    inner_embed,
    outer_experts,
    outer_dense,
    outer_small,
    outer_embed,
    moment_experts,
    moment_dense,
    moment_small,
    moment_embed,
    embed_basis,
):
    groups = lax.axis_size("rep")
    hi_prec = lax.Precision.HIGHEST

    lanes = 128
    own_shard = inner_experts[0, 0]
    halves, all_rows, my_cols = own_shard.shape
    rep_rows = all_rows // groups
    mdl_size = lax.axis_size("mdl")
    own_rows = rep_rows // mdl_size
    ex_send = (
        own_shard.reshape(halves, groups, mdl_size, own_rows, my_cols)
        .transpose(1, 2, 0, 3, 4)
        .reshape(groups, -1, lanes)
    )
    de_send = split_rows(inner_dense[0], groups).reshape(groups, -1, lanes)
    sm_send = split_rows(inner_small[0], groups).reshape(groups, -1, lanes)

    col_count = outer_embed.shape[1]
    offset = lax.axis_index("rep") * col_count
    basis_part = lax.dynamic_slice_in_dim(embed_basis, offset, col_count, 0)
    partial_value = jnp.dot(
        jnp.concatenate([outer_embed, inner_embed[0].astype(jnp.float32) * (-1.0 / groups)], axis=1),
        jnp.concatenate([basis_part, embed_basis], axis=0),
        precision=hi_prec,
        preferred_element_type=jnp.float32,
    )
    part_hi = partial_value.astype(jnp.bfloat16)
    part_lo = (partial_value - part_hi.astype(jnp.float32)).astype(jnp.bfloat16)
    pp = jnp.concatenate([part_hi.reshape(-1, lanes), part_lo.reshape(-1, lanes)])
    pp_send = jnp.broadcast_to(pp[None], (groups,) + pp.shape)

    sizes = [ex_send.shape[1], de_send.shape[1], sm_send.shape[1], pp.shape[0]]
    send = jnp.concatenate([ex_send, de_send, sm_send, pp_send], axis=1)
    first, second, raw = rep_exchange(send, pp.shape[0], groups)
    h = first.shape[0]

    def main_rows(lo, hi):
        pieces = []
        if lo < h:
            pieces.append(first[lo : min(hi, h)])
        if hi > h:
            pieces.append(second[max(lo, h) - h : hi - h])
        return pieces[0] if len(pieces) == 1 else jnp.concatenate(pieces)

    bounds = [0]
    for n in sizes[:3]:
        bounds.append(bounds[-1] + n)

    ex_sum = main_rows(bounds[0], bounds[1]).reshape(mdl_size, halves, own_rows, my_cols)
    dense_sum = main_rows(bounds[1], bounds[2]).reshape(outer_dense.shape)
    small_sum = main_rows(bounds[2], bounds[3]).reshape(outer_small.shape)
    nhalf = raw.shape[0] // 2
    coefficient = (raw[:nhalf] + raw[nhalf:]).reshape(partial_value.shape)

    expert_sum = lax.all_to_all(
        ex_sum.astype(jnp.bfloat16), "mdl", split_axis=0, concat_axis=0, tiled=True
    ).astype(jnp.float32)
    expert_sum = expert_sum.transpose(1, 2, 0, 3).reshape(outer_experts.shape[1:])
    grad_experts = outer_experts[0] - expert_sum / groups
    grad_dense = outer_dense - dense_sum / groups
    grad_small = outer_small - small_sum / groups
    grad_embed = jnp.dot(
        coefficient, basis_part.T, precision=hi_prec, preferred_element_type=jnp.float32
    )
    expert_outer, expert_moment = nesterov(outer_experts[0], moment_experts[0], grad_experts)
    dense_outer, dense_moment = nesterov(outer_dense, moment_dense, grad_dense)
    small_outer, small_moment = nesterov(outer_small, moment_small, grad_small)
    embed_outer, embed_moment = nesterov(outer_embed, moment_embed, grad_embed)
    spread = lax.all_to_all(
        expert_outer.astype(jnp.bfloat16)
        .reshape(halves, own_rows, mdl_size, my_cols)
        .transpose(2, 0, 1, 3),
        "mdl",
        split_axis=0,
        concat_axis=0,
        tiled=True,
    )

    pieces = [
        spread,
        dense_outer.astype(jnp.bfloat16),
        small_outer.astype(jnp.bfloat16),
        embed_outer.astype(jnp.bfloat16),
    ]
    flat = jnp.concatenate([p.reshape(-1, lanes) for p in pieces])
    blocks = rep_gather(flat, groups)
    outs = []
    start = 0
    for p in pieces:
        n = p.size // lanes
        g = [b[start : start + n].reshape(p.shape) for b in blocks]
        start += n
        if p.ndim == 4:
            g = jnp.concatenate(
                [x.transpose(1, 0, 2, 3).reshape(halves, rep_rows, my_cols) for x in g], axis=1
            )
        else:
            g = jnp.concatenate(g, axis=1)
        outs.append(g)

    return (
        expert_outer[None],
        expert_moment[None],
        outs[0][None],
        dense_outer,
        dense_moment,
        outs[1],
        small_outer,
        small_moment,
        outs[2],
        embed_outer,
        embed_moment,
        outs[3],
    )


def solution(mesh):
    placed = (
        P("rep", "exp", None, None, "mdl"),
        P("rep", ("exp", "mdl"), None),
        P("rep", None, None),
        P("rep", ("exp", "mdl"), None),
        P("exp", None, ("rep", "mdl"), None),
        P(("exp", "mdl"), "rep"),
        P(None, "rep"),
        P(("exp", "mdl"), "rep"),
        P("exp", None, ("rep", "mdl"), None),
        P(("exp", "mdl"), "rep"),
        P(None, "rep"),
        P(("exp", "mdl"), "rep"),
        P(),
    )
    return jax.shard_map(
        on_device,
        mesh=mesh,
        in_specs=placed,
        out_specs=(
            P("exp", None, ("rep", "mdl"), None),
            P("exp", None, ("rep", "mdl"), None),
            P("exp", None, None, "mdl"),
            P(("exp", "mdl"), "rep"),
            P(("exp", "mdl"), "rep"),
            P(("exp", "mdl"), None),
            P(None, "rep"),
            P(None, "rep"),
            P(),
            P(("exp", "mdl"), "rep"),
            P(("exp", "mdl"), "rep"),
            P(("exp", "mdl"), None),
        ),
        check_vma=False,
    )
```

```python
import jax
import jax.numpy as jnp
from jax import lax
from jax.sharding import PartitionSpec as P

decay_rate = 0.5
outer_rate = 0.7


def nesterov(outer, moment, grad_value):
    moment_new = decay_rate * moment + grad_value
    outer_new = outer - outer_rate * (grad_value + decay_rate * moment_new)
    return (outer_new, moment_new)


def split_rows(x, parts):
    rows, cols = x.shape
    return x.reshape(rows, parts, cols // parts).transpose(1, 0, 2).reshape(parts, -1)


def to_next(x, groups):
    return lax.ppermute(x, "rep", [(i, (i + 1) % groups) for i in range(groups)])


def to_prev(x, groups):
    return lax.ppermute(x, "rep", [(i, (i - 1) % groups) for i in range(groups)])


def rep_exchange(send, raw_rows, groups):
    assert groups == 4
    me = lax.axis_index("rep")
    rel = [lax.dynamic_index_in_dim(send, (me + d) % groups, 0, False) for d in range(groups)]
    k = send.shape[1]
    m = k - raw_rows
    h = m // 2
    rh = raw_rows // 2
    f32 = jnp.float32
    bf = send.dtype
    a = to_next(jnp.concatenate([rel[2][:h], rel[2][m : m + rh], rel[1][h:m], rel[1][m:]]), groups)
    b = to_prev(jnp.concatenate([rel[2][h:m], rel[2][m + rh :], rel[3][:h], rel[3][m:]]), groups)
    a_relay, a_pp_relay = a[:h], a[h : h + rh]
    a_near, a_pp = a[h + rh : h + rh + m - h], a[h + rh + m - h :]
    b_relay, b_pp_relay = b[: m - h], b[m - h : m - h + raw_rows - rh]
    b_near, b_pp = b[m - h + raw_rows - rh : m - h + raw_rows - rh + h], b[m - h + raw_rows - rh + h :]
    c = to_next(
        jnp.concatenate([(rel[1][:h].astype(f32) + a_relay.astype(f32)).astype(bf), a_pp_relay]),
        groups,
    )
    d = to_prev(
        jnp.concatenate([(rel[3][h:m].astype(f32) + b_relay.astype(f32)).astype(bf), b_pp_relay]),
        groups,
    )
    first = rel[0][:h].astype(f32) + c[:h].astype(f32) + b_near.astype(f32)
    second = rel[0][h:m].astype(f32) + a_near.astype(f32) + d[: m - h].astype(f32)
    raw = (
        rel[0][m:].astype(f32)
        + a_pp.astype(f32)
        + b_pp.astype(f32)
        + jnp.concatenate([c[h:], d[m - h :]]).astype(f32)
    )
    return jnp.concatenate([first, second, raw])


def rep_gather(flat, groups):
    assert groups == 4
    me = lax.axis_index("rep")
    n = flat.shape[0]
    half = n // 2
    from_prev = to_next(flat, groups)
    from_next = to_prev(flat, groups)
    far_a = to_next(from_prev[:half], groups)
    far_b = to_prev(from_next[half:], groups)
    far = jnp.concatenate([far_a, far_b])
    rel = [flat, from_next, far, from_prev]

    def pick(j):
        d_of_j = (j - me) % groups
        out = rel[0]
        for d in range(1, groups):
            out = jnp.where(d_of_j == d, rel[d], out)
        return out

    return [pick(j) for j in range(groups)]


def on_device(
    inner_experts,
    inner_dense,
    inner_small,
    inner_embed,
    outer_experts,
    outer_dense,
    outer_small,
    outer_embed,
    moment_experts,
    moment_dense,
    moment_small,
    moment_embed,
    embed_basis,
):
    groups = lax.axis_size("rep")
    hi_prec = lax.Precision.HIGHEST

    lanes = 128
    own_shard = inner_experts[0, 0]
    halves, all_rows, my_cols = own_shard.shape
    rep_rows = all_rows // groups
    mdl_size = lax.axis_size("mdl")
    own_rows = rep_rows // mdl_size
    ex_send = (
        own_shard.reshape(halves, groups, mdl_size, own_rows, my_cols)
        .transpose(1, 2, 0, 3, 4)
        .reshape(groups, -1, lanes)
    )
    de_send = split_rows(inner_dense[0], groups).reshape(groups, -1, lanes)
    sm_send = split_rows(inner_small[0], groups).reshape(groups, -1, lanes)

    col_count = outer_embed.shape[1]
    offset = lax.axis_index("rep") * col_count
    basis_part = lax.dynamic_slice_in_dim(embed_basis, offset, col_count, 0)
    partial_value = jnp.dot(
        jnp.concatenate([outer_embed, inner_embed[0].astype(jnp.float32) * (-1.0 / groups)], axis=1),
        jnp.concatenate([basis_part, embed_basis], axis=0),
        precision=hi_prec,
        preferred_element_type=jnp.float32,
    )
    part_hi = partial_value.astype(jnp.bfloat16)
    part_lo = (partial_value - part_hi.astype(jnp.float32)).astype(jnp.bfloat16)
    pp = jnp.concatenate([part_hi.reshape(-1, lanes), part_lo.reshape(-1, lanes)])
    pp_send = jnp.broadcast_to(pp[None], (groups,) + pp.shape)

    sizes = [ex_send.shape[1], de_send.shape[1], sm_send.shape[1], pp.shape[0]]
    send = jnp.concatenate([ex_send, de_send, sm_send, pp_send], axis=1)
    total = rep_exchange(send, pp.shape[0], groups)
    bounds = [0]
    for s in sizes:
        bounds.append(bounds[-1] + s)
    parts = [total[bounds[i] : bounds[i + 1]] for i in range(4)]

    ex_sum = parts[0].reshape(mdl_size, halves, own_rows, my_cols)
    dense_sum = parts[1].reshape(outer_dense.shape)
    small_sum = parts[2].reshape(outer_small.shape)
    nhalf = parts[3].shape[0] // 2
    coefficient = (parts[3][:nhalf] + parts[3][nhalf:]).reshape(partial_value.shape)

    expert_sum = lax.all_to_all(
        ex_sum.astype(jnp.bfloat16), "mdl", split_axis=0, concat_axis=0, tiled=True
    ).astype(jnp.float32)
    expert_sum = expert_sum.transpose(1, 2, 0, 3).reshape(outer_experts.shape[1:])
    grad_experts = outer_experts[0] - expert_sum / groups
    grad_dense = outer_dense - dense_sum / groups
    grad_small = outer_small - small_sum / groups
    grad_embed = jnp.dot(
        coefficient, basis_part.T, precision=hi_prec, preferred_element_type=jnp.float32
    )
    expert_outer, expert_moment = nesterov(outer_experts[0], moment_experts[0], grad_experts)
    dense_outer, dense_moment = nesterov(outer_dense, moment_dense, grad_dense)
    small_outer, small_moment = nesterov(outer_small, moment_small, grad_small)
    embed_outer, embed_moment = nesterov(outer_embed, moment_embed, grad_embed)
    spread = lax.all_to_all(
        expert_outer.astype(jnp.bfloat16)
        .reshape(halves, own_rows, mdl_size, my_cols)
        .transpose(2, 0, 1, 3),
        "mdl",
        split_axis=0,
        concat_axis=0,
        tiled=True,
    )

    pieces = [
        spread,
        dense_outer.astype(jnp.bfloat16),
        small_outer.astype(jnp.bfloat16),
        embed_outer.astype(jnp.bfloat16),
    ]
    flat = jnp.concatenate([p.reshape(-1, lanes) for p in pieces])
    blocks = rep_gather(flat, groups)
    outs = []
    start = 0
    for p in pieces:
        n = p.size // lanes
        g = [b[start : start + n].reshape(p.shape) for b in blocks]
        start += n
        if p.ndim == 4:
            g = jnp.concatenate(
                [x.transpose(1, 0, 2, 3).reshape(halves, rep_rows, my_cols) for x in g], axis=1
            )
        else:
            g = jnp.concatenate(g, axis=1)
        outs.append(g)

    return (
        expert_outer[None],
        expert_moment[None],
        outs[0][None],
        dense_outer,
        dense_moment,
        outs[1],
        small_outer,
        small_moment,
        outs[2],
        embed_outer,
        embed_moment,
        outs[3],
    )


def solution(mesh):
    placed = (
        P("rep", "exp", None, None, "mdl"),
        P("rep", ("exp", "mdl"), None),
        P("rep", None, None),
        P("rep", ("exp", "mdl"), None),
        P("exp", None, ("rep", "mdl"), None),
        P(("exp", "mdl"), "rep"),
        P(None, "rep"),
        P(("exp", "mdl"), "rep"),
        P("exp", None, ("rep", "mdl"), None),
        P(("exp", "mdl"), "rep"),
        P(None, "rep"),
        P(("exp", "mdl"), "rep"),
        P(),
    )
    return jax.shard_map(
        on_device,
        mesh=mesh,
        in_specs=placed,
        out_specs=(
            P("exp", None, ("rep", "mdl"), None),
            P("exp", None, ("rep", "mdl"), None),
            P("exp", None, None, "mdl"),
            P(("exp", "mdl"), "rep"),
            P(("exp", "mdl"), "rep"),
            P(("exp", "mdl"), None),
            P(None, "rep"),
            P(None, "rep"),
            P(),
            P(("exp", "mdl"), "rep"),
            P(("exp", "mdl"), "rep"),
            P(("exp", "mdl"), None),
        ),
        check_vma=False,
    )
```
